128 devices in a mesh: dp: 2 (over y_hi), pipe: 4 (over y_lo, core), chan: 16 (over x, z).
Axes of the slice: x: 4, y: 4 (y_hi: 2, y_lo: 2; y = y_hi * 2 + y_lo), z: 4, core: 2. Of those that a mesh axis runs over, the one named last changes fastest.
Arguments:
- latents: bfloat16 [2, 4, 640, 512], P('dp', None, 'chan'), may hold values from -6 to 6
- cotangent: bfloat16 [2, 4, 640, 512], P('dp', None, 'chan'), may hold values from -6 to 6
- order: int32 [2, 4], P('dp'), may hold values from 0 to 3, each once within a row
- tstep: int32 [2, 4], P('dp'), may hold values from 0 to 999
- emb_table: float32 [1000, 4, 640], P(None, None, 'chan'), may hold values from -5 to 5
- gn_gain: float32 [4, 640], P(None, 'chan'), may hold values from 0.1 to 1.9
- weights: bfloat16 [4, 27, 640, 640], P(None, None, 'chan'), may hold values from -0.0625 to 0.0625
Outputs:
- grad_weights: float32 [4, 27, 640, 640], P('pipe', None, 'chan')
The draws below stay inside these ranges and needn't reach their ends.
Inputs may be any that keep to these rules, and one draw needn't show every extreme that they name: Each row of order names every micro-batch once.
All inputs are finite; a program needn't handle non-finite values.
Results may differ from the reference program's by a relative error of at most 0.015.
Values may be sent and summed in bfloat16 or wider, within the bound.
No kernel may reach another device: no remote copies, remote signals or barrier semaphores. Data moves between devices by JAX's collectives and lax.ppermute only.
A program may use at most 128 MiB of HBM per device.

```python
from functools import partial
import jax
import jax.numpy as jnp
from jax import lax

C = 640
GROUPS = 32
FR = 2
HT = 16
WD = 16
TSTEPS = 1000
SECTIONS = 4
REPLICAS = 2
NMB = 4
CELLS = 512
CH_DEV = 40


def plant(values, stream_key, smallest, top_value):
    longest = values.shape.index(max(values.shape))
    spots = []
    for shift in (0, 1):
        where = [jax.random.randint(jax.random.fold_in(stream_key, axis), (), 0, length) for axis, length in enumerate(values.shape)]
        where[longest] = (where[longest] + shift) % values.shape[longest]
        spots.append(tuple(where))
    return values.at[spots[0]].set(smallest).at[spots[1]].set(top_value)


def strengthened(entries, key, source, target, shards_of, factor):
    owner, partner = [(jnp.arange(entries.shape[dim]) // (entries.shape[dim] // shards_of)).reshape([-1 if axis == dim else 1 for axis in range(entries.ndim)]) for dim in (source, target)]
    chosen = jax.random.permutation(key, shards_of)[partner]
    strong = (owner == chosen) | (owner == (partner + shards_of // 2) % shards_of)
    return jnp.where(strong, factor * entries, entries)


def block_scale(own_key, extent, cuts, least, largest):
    level, own = 1.0, jax.random.fold_in(own_key, 6)
    for axis_at, blocks in cuts:
        steps = jnp.exp(jax.random.uniform(jax.random.fold_in(own, axis_at), (blocks,), jnp.float32, least / len(cuts), largest / len(cuts)))
        level = level * jnp.repeat(steps, extent[axis_at] // blocks).reshape([-1 if axis == axis_at else 1 for axis in range(len(extent))])
    return level


def scatter_about(rng, extent, scale, reach, split=(), kind=jnp.bfloat16):
    loudness = block_scale(rng, extent, split, -0.22, 0.18) if split else 1.0
    array = jax.random.normal(rng, extent, jnp.float32) * scale * loudness
    return jnp.minimum(jnp.maximum(array, -reach), reach).astype(kind)


def bell_draw_with(key, extent, deviation, most, split, heavy, held_as=jnp.bfloat16):
    entries = deviation * jax.random.normal(key, extent, jnp.float32)
    if split:
        entries = entries * block_scale(key, extent, split, -0.22, 0.18)
    return jnp.clip(strengthened(entries, jax.random.fold_in(key, 3), *heavy), -most, most).astype(held_as)


def setup_inputs(seed: int = 0) -> dict:
    key_of = jax.random.split(jax.random.key(seed), 8)
    latents = scatter_about(key_of[0], (REPLICAS, NMB, C, CELLS), 1.0, 6.0, ((0, 2), (2, 16)))
    cotangent = scatter_about(key_of[1], (REPLICAS, NMB, C, CELLS), 1.0, 6.0, ((0, 2), (2, 16)))
    order = jax.vmap(lambda own: jax.random.permutation(own, NMB))(jax.random.split(key_of[2], REPLICAS)).reshape((REPLICAS, NMB)).astype(jnp.int32)
    tstep = plant(jax.random.randint(key_of[3], (REPLICAS, NMB), 0, TSTEPS), jax.random.fold_in(key_of[3], 1), 0, TSTEPS - 1).astype(jnp.int32)
    emb_table = scatter_about(key_of[4], (TSTEPS, SECTIONS, C), 1.0, 5.0, ((2, 16),), jnp.float32)
    gn_gain = jnp.clip(1.0 + 0.18 * jax.random.normal(key_of[5], (SECTIONS, C), jnp.float32), 0.1, 1.9)
    weights = bell_draw_with(key_of[6], (SECTIONS, 27, C, C), (27 * C) ** -0.5, 0.0625, ((2, 16),), (2, 3, 16, 2.0))
    return dict(latents=latents, cotangent=cotangent, order=order, tstep=tstep, emb_table=emb_table, gn_gain=gn_gain, weights=weights)


EPSILON = 1e-05

def pre_act(field, gain, offset):
    channels, places = field.shape
    grouped = field.reshape(channels // (C // GROUPS), -1)
    centred = grouped - lax.optimization_barrier(jnp.mean(grouped, axis=1, keepdims=True))
    spread = lax.optimization_barrier(jnp.mean(centred * centred, axis=1, keepdims=True))
    normed = (centred * lax.rsqrt(spread + EPSILON)).reshape(channels, places)
    return jax.nn.silu(normed * gain[:, None] + offset[:, None])

def tap_stack(field):
    places = field.shape[1]
    plane = HT * WD
    margin = plane + WD + 1
    padded = jnp.pad(field, ((0, 0), (margin, margin)))
    position = jnp.arange(places, dtype=jnp.int32)
    frame_at = position // plane
    line_at = position // WD % HT
    column_at = position % WD
    pieces = []
    for shift_f in (-1, 0, 1):
        for shift_h in (-1, 0, 1):
            for shift_w in (-1, 0, 1):
                offset = shift_f * plane + shift_h * WD + shift_w
                inside = (frame_at + shift_f >= 0) & (frame_at + shift_f < FR)
                inside = inside & (line_at + shift_h >= 0) & (line_at + shift_h < HT)
                inside = inside & (column_at + shift_w >= 0) & (column_at + shift_w < WD)
                moved = lax.slice_in_dim(padded, margin + offset, margin + offset + places, axis=1)
                pieces.append(jnp.where(inside[None, :], moved, jnp.zeros_like(moved)))
    return jnp.concatenate(pieces, axis=0)

def tap_adjoint(grads, channels, places):
    pull = jax.vjp(tap_stack, jnp.zeros((channels, places), jnp.float32))[1]
    return pull(grads)[0]

def section_forward(field, weight, gain, offset):
    active = pre_act(field.astype(jnp.float32), gain, offset).astype(jnp.bfloat16)
    total = jnp.zeros((C, CELLS), jnp.float32)
    for member in range(C // CH_DEV):
        front = tap_stack(active[member * CH_DEV:(member + 1) * CH_DEV])
        rows_block = weight[:, member * CH_DEV:(member + 1) * CH_DEV, :].reshape(27 * CH_DEV, C)
        part = lax.dot_general(rows_block, front, (((0,), (0,)), ((), ())), preferred_element_type=jnp.float32)
        rounded = lax.optimization_barrier(part.astype(jnp.bfloat16))
        total = total + rounded.astype(jnp.float32)
    return (field.astype(jnp.float32) + total).astype(jnp.bfloat16)

def section_backward(field, grad, weight, gain, offset):
    active, pull = jax.vjp(partial(pre_act, gain=gain, offset=offset), field.astype(jnp.float32))
    front = tap_stack(active.astype(jnp.bfloat16))
    weight_rows = weight.reshape(27 * C, C)
    grad_taps = jnp.dot(weight_rows, grad, preferred_element_type=jnp.float32)
    grad_weight = lax.dot_general(front, grad, (((1,), (1,)), ((), ())), preferred_element_type=jnp.float32)
    grad_field = grad.astype(jnp.float32) + pull(tap_adjoint(grad_taps, C, CELLS))[0]
    return (grad_field.astype(jnp.bfloat16), grad_weight.reshape(27, C, C))

def reference(latents, cotangent, order, tstep, emb_table, gn_gain, weights):
    grads = jnp.zeros((SECTIONS, 27, C, C), jnp.float32)
    for replica in range(REPLICAS):
        for slot_index in range(NMB):
            sample = order[replica, slot_index]
            timestep = tstep[replica, sample]
            field = latents[replica, sample]
            saved = []
            for section in range(SECTIONS):
                saved.append(field)
                field = section_forward(field, weights[section], gn_gain[section], emb_table[timestep, section])
            grad = cotangent[replica, slot_index]
            for section in reversed(range(SECTIONS)):
                grad, part = section_backward(saved[section], grad, weights[section], gn_gain[section], emb_table[timestep, section])
                grads = grads.at[section].add(part)
    return grads
```

```python
from functools import partial

import jax
import jax.numpy as jnp
from jax import lax
from jax.sharding import PartitionSpec as P

C = 640
GROUPS = 32
FR = 2
HT = 16
WD = 16


EPSILON = 1e-05


def passed_along(value, axis, steps):
    count = lax.axis_size(axis)
    first, last = (max(0, -steps), min(count, count - steps))
    return lax.ppermute(value, axis, [(source, source + steps) for source in range(first, last)])


def from_partner(value, axis, apart):
    mask = 2**apart
    pairs = [(source, source ^ mask) for source in range(lax.axis_size(axis))]
    return lax.ppermute(value, axis, pairs)


def pre_act(field, gain, offset):
    channels, places = field.shape
    grouped = field.reshape(channels // (C // GROUPS), -1)
    centred = grouped - jnp.mean(grouped, axis=1, keepdims=True)
    spread = jnp.mean(centred * centred, axis=1, keepdims=True)
    normed = (centred * lax.rsqrt(spread + EPSILON)).reshape(channels, places)
    return jax.nn.silu(normed * gain[:, None] + offset[:, None])


def tap_stack(field):
    places = field.shape[1]
    plane = HT * WD
    margin = plane + WD + 1
    padded = jnp.pad(field, ((0, 0), (margin, margin)))
    position = jnp.arange(places, dtype=jnp.int32)
    frame_at = position // plane
    line_at = position // WD % HT
    column_at = position % WD
    pieces = []
    for shift_f in (-1, 0, 1):
        for shift_h in (-1, 0, 1):
            for shift_w in (-1, 0, 1):
                offset = shift_f * plane + shift_h * WD + shift_w
                inside = (frame_at + shift_f >= 0) & (frame_at + shift_f < FR)
                inside = inside & (line_at + shift_h >= 0) & (line_at + shift_h < HT)
                inside = inside & (column_at + shift_w >= 0) & (column_at + shift_w < WD)
                moved = lax.slice_in_dim(padded, margin + offset, margin + offset + places, axis=1)
                pieces.append(jnp.where(inside[None, :], moved, jnp.zeros_like(moved)))
    return jnp.concatenate(pieces, axis=0)


def tap_adjoint(grads, channels, places):
    pull = jax.vjp(tap_stack, jnp.zeros((channels, places), jnp.float32))[1]
    return pull(grads)[0]


def partial_term(weight_rows, front):
    return lax.dot_general(
        weight_rows, front, (((0,), (0,)), ((), ())), preferred_element_type=jnp.float32
    )


def conv_sums(rows_pair, fronts_pair):
    count = lax.axis_size("chan")
    parts = jnp.stack(
        [
            partial_term(rows, front).astype(jnp.bfloat16)
            for rows, front in zip(rows_pair, fronts_pair)
        ]
    )
    parts = parts.reshape(parts.shape[0], count, parts.shape[1] // count, parts.shape[2])
    got = lax.all_to_all(parts, "chan", 1, 1, tiled=False)
    sums = jnp.sum(got.astype(jnp.float32), axis=1)
    return [sums[direction] for direction in range(sums.shape[0])]


def gather_pair(grads_pair):
    count = lax.axis_size("chan")
    stacked = jnp.stack(grads_pair)
    spread = jnp.broadcast_to(stacked[:, None], (stacked.shape[0], count) + stacked.shape[1:])
    got = lax.all_to_all(spread, "chan", 1, 1, tiled=False)
    got = got.reshape(got.shape[0], count * got.shape[2], got.shape[3])
    return [got[direction] for direction in range(got.shape[0])]


def fold_grads(grad_taps, grad_weight, piece, weight_rows, front):
    grad_taps = jnp.dot(weight_rows, piece, preferred_element_type=jnp.float32)
    previous = grad_weight
    update = lax.dot_general(
        front, piece, (((1,), (1,)), ((), ())), preferred_element_type=jnp.float32
    )
    grad_weight = previous + update
    return (grad_taps, grad_weight)


def grad_fold(full_grad, weight_rows, front, grad_weight):
    empty = jnp.zeros(front.shape, jnp.float32)
    return fold_grads(empty, grad_weight, full_grad, weight_rows, front)


def per_device(latents, cotangent, order, tstep, emb_table, gn_gain, weights):
    pipe_count = lax.axis_size("pipe")
    section_rank = lax.axis_index("pipe")
    mirror_rank = pipe_count - 1 - section_rank
    channels = latents.shape[2]
    places = latents.shape[3]
    slot_count = latents.shape[1]
    half_slots = slot_count // 2
    width = weights.shape[3]
    order_row = order[0]
    timestep_row = tstep[0]
    slot_ids = jnp.arange(slot_count, dtype=jnp.int32)
    picked = jnp.sum(
        jnp.where(order_row[:, None] == slot_ids[None, :], timestep_row[None, :], 0), axis=1
    )
    step_ids = jnp.arange(emb_table.shape[0], dtype=jnp.int32)
    one_hot = (picked[:, None] == step_ids[None, :]).astype(jnp.float32)
    entries_all = jnp.take(latents[0], order_row, axis=0)
    sections = (section_rank, mirror_rank)
    rows_list = []
    gains = []
    offsets_list = []
    inputs = []
    cotans = []
    for direction in range(2):
        section = sections[direction]
        rows_list.append(
            lax.dynamic_index_in_dim(weights, section, 0, keepdims=False).reshape(
                27 * channels, width
            )
        )
        gains.append(lax.dynamic_index_in_dim(gn_gain, section, 0, keepdims=False))
        table = lax.dynamic_index_in_dim(emb_table, section, 1, keepdims=False)
        hot_rows = one_hot[direction * half_slots : (direction + 1) * half_slots]
        offsets_list.append(jnp.dot(hot_rows, table, precision=lax.Precision.HIGHEST))
        inputs.append(entries_all[direction * half_slots : (direction + 1) * half_slots])
        cotans.append(cotangent[0, direction * half_slots : (direction + 1) * half_slots])
    ticks = pipe_count + half_slots - 1
    zero_field = jnp.zeros((channels, places), jnp.bfloat16)
    received = [zero_field, zero_field]
    stores = [jnp.zeros((half_slots, channels, places), jnp.bfloat16) for direction in range(2)]
    for tick_index in range(ticks):
        fronts = []
        entries_now = []
        for direction in range(2):
            section = sections[direction]
            micro = tick_index - section
            is_live = (micro >= 0) & (micro < half_slots)
            clipped = jnp.clip(micro, 0, half_slots - 1)
            fresh = lax.dynamic_index_in_dim(inputs[direction], clipped, 0, keepdims=False)
            entry = jnp.where(section == 0, fresh, received[direction])
            kept = lax.dynamic_index_in_dim(stores[direction], clipped, 0, keepdims=False)
            stores[direction] = lax.dynamic_update_index_in_dim(
                stores[direction], jnp.where(is_live, entry, kept), clipped, 0
            )
            offset = lax.dynamic_index_in_dim(offsets_list[direction], clipped, 0, keepdims=False)
            active = pre_act(entry.astype(jnp.float32), gains[direction], offset).astype(
                jnp.bfloat16
            )
            fronts.append(tap_stack(active))
            entries_now.append(entry)
        sums = conv_sums(rows_list, fronts)
        results = [
            (entries_now[direction].astype(jnp.float32) + sums[direction]).astype(jnp.bfloat16)
            for direction in range(2)
        ]
        if tick_index + 1 < ticks:
            received = [passed_along(results[0], "pipe", 1), passed_along(results[1], "pipe", -1)]
    grads_in = [zero_field, zero_field]
    accums = [jnp.zeros((27 * channels, width), jnp.float32) for direction in range(2)]
    for tick_index in range(ticks):
        live_grads = []
        fronts = []
        pullers = []
        for direction in range(2):
            section = sections[direction]
            micro = tick_index - (pipe_count - 1 - section)
            is_live = (micro >= 0) & (micro < half_slots)
            clipped = jnp.clip(micro, 0, half_slots - 1)
            fresh = lax.dynamic_index_in_dim(cotans[direction], clipped, 0, keepdims=False)
            incoming = jnp.where(section == pipe_count - 1, fresh, grads_in[direction])
            live_grads.append(jnp.where(is_live, incoming, zero_field))
            entry = lax.dynamic_index_in_dim(stores[direction], clipped, 0, keepdims=False)
            offset = lax.dynamic_index_in_dim(offsets_list[direction], clipped, 0, keepdims=False)
            active, pull = jax.vjp(
                partial(pre_act, gain=gains[direction], offset=offset), entry.astype(jnp.float32)
            )
            fronts.append(tap_stack(active.astype(jnp.bfloat16)))
            pullers.append(pull)
        full_grads = gather_pair(live_grads)
        folded = [
            grad_fold(
                full_grads[direction], rows_list[direction], fronts[direction], accums[direction]
            )
            for direction in range(2)
        ]
        sends = []
        for direction in range(2):
            grad_taps, accums[direction] = folded[direction]
            back = pullers[direction](tap_adjoint(grad_taps, channels, places))[0]
            sends.append((live_grads[direction].astype(jnp.float32) + back).astype(jnp.bfloat16))
        if tick_index + 1 < ticks:
            grads_in = [passed_along(sends[0], "pipe", -1), passed_along(sends[1], "pipe", 1)]
    mirrored = accums[1]
    for bit_index in range(pipe_count.bit_length() - 1):
        mirrored = from_partner(mirrored.astype(jnp.bfloat16), "pipe", bit_index).astype(
            mirrored.dtype
        )
    combined = accums[0] + mirrored
    total = lax.psum(combined.astype(jnp.bfloat16), "dp").astype(jnp.float32)
    return total.reshape(1, 27, channels, width)


def solution(mesh):
    return jax.shard_map(
        per_device,
        mesh=mesh,
        in_specs=(
            P("dp", None, "chan", None),
            P("dp", None, "chan", None),
            P("dp", None),
            P("dp", None),
            P(None, None, "chan"),
            P(None, "chan"),
            P(None, None, "chan", None),
        ),
        out_specs=P("pipe", None, "chan", None),
        check_vma=False,
    )
```

```python
from functools import partial

import jax
import jax.numpy as jnp
from jax import lax
from jax.sharding import PartitionSpec as P

C = 640
GROUPS = 32
FR = 2
HT = 16
WD = 16


EPSILON = 1e-05


def passed_along(value, axis, steps):
    count = lax.axis_size(axis)
    first, last = (max(0, -steps), min(count, count - steps))
    return lax.ppermute(value, axis, [(source, source + steps) for source in range(first, last)])


def from_partner(value, axis, apart):
    mask = 2**apart
    pairs = [(source, source ^ mask) for source in range(lax.axis_size(axis))]
    return lax.ppermute(value, axis, pairs)


def ring_pairs(replica_count, pipe_count):
    pairs = []
    for replica in range(replica_count):
        for rank in range(pipe_count):
            step = 1 if rank >= pipe_count // 2 else 0
            target = ((replica + step) % replica_count) * pipe_count + pipe_count - 1 - rank
            pairs.append((replica * pipe_count + rank, target))
    return pairs


def ring_pass(value, pairs):
    moved = lax.ppermute(value.astype(jnp.bfloat16), ("dp", "pipe"), pairs)
    return moved.astype(jnp.float32)


def pre_act(field, gain, offset):
    channels, places = field.shape
    grouped = field.reshape(channels // (C // GROUPS), -1)
    centred = grouped - jnp.mean(grouped, axis=1, keepdims=True)
    spread = jnp.mean(centred * centred, axis=1, keepdims=True)
    normed = (centred * lax.rsqrt(spread + EPSILON)).reshape(channels, places)
    return jax.nn.silu(normed * gain[:, None] + offset[:, None])


def tap_stack(field):
    places = field.shape[1]
    plane = HT * WD
    margin = plane + WD + 1
    padded = jnp.pad(field, ((0, 0), (margin, margin)))
    position = jnp.arange(places, dtype=jnp.int32)
    frame_at = position // plane
    line_at = position // WD % HT
    column_at = position % WD
    pieces = []
    for shift_f in (-1, 0, 1):
        for shift_h in (-1, 0, 1):
            for shift_w in (-1, 0, 1):
                offset = shift_f * plane + shift_h * WD + shift_w
                inside = (frame_at + shift_f >= 0) & (frame_at + shift_f < FR)
                inside = inside & (line_at + shift_h >= 0) & (line_at + shift_h < HT)
                inside = inside & (column_at + shift_w >= 0) & (column_at + shift_w < WD)
                moved = lax.slice_in_dim(padded, margin + offset, margin + offset + places, axis=1)
                pieces.append(jnp.where(inside[None, :], moved, jnp.zeros_like(moved)))
    return jnp.concatenate(pieces, axis=0)


def tap_adjoint(grads, channels, places):
    pull = jax.vjp(tap_stack, jnp.zeros((channels, places), jnp.float32))[1]
    return pull(grads)[0]


def partial_term(weight_rows, front):
    return lax.dot_general(
        weight_rows, front, (((0,), (0,)), ((), ())), preferred_element_type=jnp.float32
    )


def conv_sums(rows_pair, fronts_pair):
    count = lax.axis_size("chan")
    parts = jnp.stack(
        [
            partial_term(rows, front).astype(jnp.bfloat16)
            for rows, front in zip(rows_pair, fronts_pair)
        ]
    )
    parts = parts.reshape(parts.shape[0], count, parts.shape[1] // count, parts.shape[2])
    got = lax.all_to_all(parts, "chan", 1, 1, tiled=False)
    sums = jnp.sum(got.astype(jnp.float32), axis=1)
    return [sums[direction] for direction in range(sums.shape[0])]


def gather_pair(grads_pair):
    count = lax.axis_size("chan")
    stacked = jnp.stack(grads_pair)
    spread = jnp.broadcast_to(stacked[:, None], (stacked.shape[0], count) + stacked.shape[1:])
    got = lax.all_to_all(spread, "chan", 1, 1, tiled=False)
    got = got.reshape(got.shape[0], count * got.shape[2], got.shape[3])
    return [got[direction] for direction in range(got.shape[0])]


def fold_grads(grad_taps, grad_weight, piece, weight_rows, front):
    grad_taps = jnp.dot(weight_rows, piece, preferred_element_type=jnp.float32)
    previous = grad_weight
    update = lax.dot_general(
        front, piece, (((1,), (1,)), ((), ())), preferred_element_type=jnp.float32
    )
    grad_weight = previous + update
    return (grad_taps, grad_weight)


def grad_fold(full_grad, weight_rows, front, grad_weight):
    empty = jnp.zeros(front.shape, jnp.float32)
    return fold_grads(empty, grad_weight, full_grad, weight_rows, front)


def per_device(latents, cotangent, order, tstep, emb_table, gn_gain, weights):
    pipe_count = lax.axis_size("pipe")
    section_rank = lax.axis_index("pipe")
    mirror_rank = pipe_count - 1 - section_rank
    channels = latents.shape[2]
    places = latents.shape[3]
    slot_count = latents.shape[1]
    half_slots = slot_count // 2
    width = weights.shape[3]
    order_row = order[0]
    timestep_row = tstep[0]
    slot_ids = jnp.arange(slot_count, dtype=jnp.int32)
    picked = jnp.sum(
        jnp.where(order_row[:, None] == slot_ids[None, :], timestep_row[None, :], 0), axis=1
    )
    step_ids = jnp.arange(emb_table.shape[0], dtype=jnp.int32)
    one_hot = (picked[:, None] == step_ids[None, :]).astype(jnp.float32)
    entries_all = jnp.take(latents[0], order_row, axis=0)
    sections = (section_rank, mirror_rank)
    rows_list = []
    gains = []
    offsets_list = []
    inputs = []
    cotans = []
    for direction in range(2):
        section = sections[direction]
        rows_list.append(
            lax.dynamic_index_in_dim(weights, section, 0, keepdims=False).reshape(
                27 * channels, width
            )
        )
        gains.append(lax.dynamic_index_in_dim(gn_gain, section, 0, keepdims=False))
        table = lax.dynamic_index_in_dim(emb_table, section, 1, keepdims=False)
        hot_rows = one_hot[direction * half_slots : (direction + 1) * half_slots]
        offsets_list.append(jnp.dot(hot_rows, table, precision=lax.Precision.HIGHEST))
        inputs.append(entries_all[direction * half_slots : (direction + 1) * half_slots])
        cotans.append(cotangent[0, direction * half_slots : (direction + 1) * half_slots])
    ticks = pipe_count + half_slots - 1
    zero_field = jnp.zeros((channels, places), jnp.bfloat16)
    received = [zero_field, zero_field]
    stores = [jnp.zeros((half_slots, channels, places), jnp.bfloat16) for direction in range(2)]
    for tick_index in range(ticks):
        fronts = []
        entries_now = []
        for direction in range(2):
            section = sections[direction]
            micro = tick_index - section
            is_live = (micro >= 0) & (micro < half_slots)
            clipped = jnp.clip(micro, 0, half_slots - 1)
            fresh = lax.dynamic_index_in_dim(inputs[direction], clipped, 0, keepdims=False)
            entry = jnp.where(section == 0, fresh, received[direction])
            kept = lax.dynamic_index_in_dim(stores[direction], clipped, 0, keepdims=False)
            stores[direction] = lax.dynamic_update_index_in_dim(
                stores[direction], jnp.where(is_live, entry, kept), clipped, 0
            )
            offset = lax.dynamic_index_in_dim(offsets_list[direction], clipped, 0, keepdims=False)
            active = pre_act(entry.astype(jnp.float32), gains[direction], offset).astype(
                jnp.bfloat16
            )
            fronts.append(tap_stack(active))
            entries_now.append(entry)
        sums = conv_sums(rows_list, fronts)
        results = [
            (entries_now[direction].astype(jnp.float32) + sums[direction]).astype(jnp.bfloat16)
            for direction in range(2)
        ]
        if tick_index + 1 < ticks:
            received = [passed_along(results[0], "pipe", 1), passed_along(results[1], "pipe", -1)]
    grads_in = [zero_field, zero_field]
    accums = [jnp.zeros((27 * channels, width), jnp.float32) for direction in range(2)]
    for tick_index in range(ticks):
        live_grads = []
        fronts = []
        pullers = []
        for direction in range(2):
            section = sections[direction]
            micro = tick_index - (pipe_count - 1 - section)
            is_live = (micro >= 0) & (micro < half_slots)
            clipped = jnp.clip(micro, 0, half_slots - 1)
            fresh = lax.dynamic_index_in_dim(cotans[direction], clipped, 0, keepdims=False)
            incoming = jnp.where(section == pipe_count - 1, fresh, grads_in[direction])
            live_grads.append(jnp.where(is_live, incoming, zero_field))
            entry = lax.dynamic_index_in_dim(stores[direction], clipped, 0, keepdims=False)
            offset = lax.dynamic_index_in_dim(offsets_list[direction], clipped, 0, keepdims=False)
            active, pull = jax.vjp(
                partial(pre_act, gain=gains[direction], offset=offset), entry.astype(jnp.float32)
            )
            fronts.append(tap_stack(active.astype(jnp.bfloat16)))
            pullers.append(pull)
        full_grads = gather_pair(live_grads)
        folded = [
            grad_fold(
                full_grads[direction], rows_list[direction], fronts[direction], accums[direction]
            )
            for direction in range(2)
        ]
        sends = []
        for direction in range(2):
            grad_taps, accums[direction] = folded[direction]
            back = pullers[direction](tap_adjoint(grad_taps, channels, places))[0]
            sends.append((live_grads[direction].astype(jnp.float32) + back).astype(jnp.bfloat16))
        if tick_index + 1 < ticks:
            grads_in = [passed_along(sends[0], "pipe", -1), passed_along(sends[1], "pipe", 1)]
    replica_count = lax.axis_size("dp")
    onward = ring_pairs(replica_count, pipe_count)
    backward_pairs = [(target, source) for source, target in onward]
    half = width // 2
    own, other = accums
    own_a, own_b = own[:, :half], own[:, half:]
    other_a, other_b = other[:, :half], other[:, half:]
    from_pred = ring_pass(jnp.concatenate([own_a, other_b], axis=1), onward)
    from_succ = ring_pass(jnp.concatenate([other_a, own_b], axis=1), backward_pairs)
    own_a = own_a + from_succ[:, :half]
    other_a = other_a + from_pred[:, :half]
    own_b = own_b + from_pred[:, half:]
    other_b = other_b + from_succ[:, half:]
    final_a = own_a + ring_pass(other_a, onward)
    final_b = own_b + ring_pass(other_b, backward_pairs)
    total = jnp.concatenate([final_a, final_b], axis=1)
    return total.reshape(1, 27, channels, width)


def solution(mesh):
    return jax.shard_map(
        per_device,
        mesh=mesh,
        in_specs=(
            P("dp", None, "chan", None),
            P("dp", None, "chan", None),
            P("dp", None),
            P("dp", None),
            P(None, None, "chan"),
            P(None, "chan"),
            P(None, None, "chan", None),
        ),
        out_specs=P("pipe", None, "chan", None),
        check_vma=False,
    )
```

```python
from functools import partial

import jax
import jax.numpy as jnp
from jax import lax
from jax.sharding import PartitionSpec as P

C = 640
GROUPS = 32
FR = 2
HT = 16
WD = 16


EPSILON = 1e-05


def passed_along(value, axis, steps):
    count = lax.axis_size(axis)
    first, last = (max(0, -steps), min(count, count - steps))
    return lax.ppermute(value, axis, [(source, source + steps) for source in range(first, last)])


def from_partner(value, axis, apart):
    mask = 2**apart
    pairs = [(source, source ^ mask) for source in range(lax.axis_size(axis))]
    return lax.ppermute(value, axis, pairs)


def ring_pairs(replica_count, pipe_count):
    pairs = []
    for replica in range(replica_count):
        for rank in range(pipe_count):
            step = 1 if rank >= pipe_count // 2 else 0
            target = ((replica + step) % replica_count) * pipe_count + pipe_count - 1 - rank
            pairs.append((replica * pipe_count + rank, target))
    return pairs


def ring_pass(value, pairs):
    moved = lax.ppermute(value.astype(jnp.bfloat16), ("dp", "pipe"), pairs)
    return moved.astype(jnp.float32)


def pre_act(field, gain, offset):
    channels, places = field.shape
    grouped = field.reshape(channels // (C // GROUPS), -1)
    centred = grouped - jnp.mean(grouped, axis=1, keepdims=True)
    spread = jnp.mean(centred * centred, axis=1, keepdims=True)
    normed = (centred * lax.rsqrt(spread + EPSILON)).reshape(channels, places)
    return jax.nn.silu(normed * gain[:, None] + offset[:, None])


def tap_stack(field):
    places = field.shape[1]
    plane = HT * WD
    margin = plane + WD + 1
    padded = jnp.pad(field, ((0, 0), (margin, margin)))
    position = jnp.arange(places, dtype=jnp.int32)
    frame_at = position // plane
    line_at = position // WD % HT
    column_at = position % WD
    pieces = []
    for shift_f in (-1, 0, 1):
        for shift_h in (-1, 0, 1):
            for shift_w in (-1, 0, 1):
                offset = shift_f * plane + shift_h * WD + shift_w
                inside = (frame_at + shift_f >= 0) & (frame_at + shift_f < FR)
                inside = inside & (line_at + shift_h >= 0) & (line_at + shift_h < HT)
                inside = inside & (column_at + shift_w >= 0) & (column_at + shift_w < WD)
                moved = lax.slice_in_dim(padded, margin + offset, margin + offset + places, axis=1)
                pieces.append(jnp.where(inside[None, :], moved, jnp.zeros_like(moved)))
    return jnp.concatenate(pieces, axis=0)


def tap_adjoint(grads, channels, places):
    pull = jax.vjp(tap_stack, jnp.zeros((channels, places), jnp.float32))[1]
    return pull(grads)[0]


def partial_term(weight_rows, front):
    return lax.dot_general(
        weight_rows, front, (((0,), (0,)), ((), ())), preferred_element_type=jnp.float32
    )


def conv_sums(rows_pair, fronts_pair):
    count = lax.axis_size("chan")
    parts = jnp.stack(
        [
            partial_term(rows, front).astype(jnp.bfloat16)
            for rows, front in zip(rows_pair, fronts_pair)
        ]
    )
    parts = parts.reshape(parts.shape[0], count, parts.shape[1] // count, parts.shape[2])
    got = lax.all_to_all(parts, "chan", 1, 1, tiled=False)
    sums = jnp.sum(got.astype(jnp.float32), axis=1)
    return [sums[direction] for direction in range(sums.shape[0])]


def conv_sum_single(rows_pair, fronts_pair, first_live):
    count = lax.axis_size("chan")
    first, second = [
        partial_term(rows, front).astype(jnp.bfloat16)
        for rows, front in zip(rows_pair, fronts_pair)
    ]
    part = jnp.where(first_live, first, second)
    part = part.reshape(count, part.shape[0] // count, part.shape[1])
    got = lax.all_to_all(part, "chan", 0, 0, tiled=False)
    total = jnp.sum(got.astype(jnp.float32), axis=0)
    return [total, total]


def gather_single(grads_pair, live_pair):
    count = lax.axis_size("chan")
    merged = grads_pair[0] + grads_pair[1]
    spread = jnp.broadcast_to(merged[None], (count,) + merged.shape)
    got = lax.all_to_all(spread, "chan", 0, 0, tiled=False)
    got = got.reshape(count * got.shape[1], got.shape[2])
    return [jnp.where(live, got, jnp.zeros_like(got)) for live in live_pair]


def both_live(tick_index, pipe_count, half_slots, backward):
    for rank in range(pipe_count):
        first = tick_index - (pipe_count - 1 - rank if backward else rank)
        second = tick_index - (rank if backward else pipe_count - 1 - rank)
        if 0 <= first < half_slots and 0 <= second < half_slots:
            return True
    return False


def gather_pair(grads_pair):
    count = lax.axis_size("chan")
    stacked = jnp.stack(grads_pair)
    spread = jnp.broadcast_to(stacked[:, None], (stacked.shape[0], count) + stacked.shape[1:])
    got = lax.all_to_all(spread, "chan", 1, 1, tiled=False)
    got = got.reshape(got.shape[0], count * got.shape[2], got.shape[3])
    return [got[direction] for direction in range(got.shape[0])]


def fold_grads(grad_taps, grad_weight, piece, weight_rows, front):
    grad_taps = jnp.dot(weight_rows, piece, preferred_element_type=jnp.float32)
    previous = grad_weight
    update = lax.dot_general(
        front, piece, (((1,), (1,)), ((), ())), preferred_element_type=jnp.float32
    )
    grad_weight = previous + update
    return (grad_taps, grad_weight)


def grad_fold(full_grad, weight_rows, front, grad_weight):
    empty = jnp.zeros(front.shape, jnp.float32)
    return fold_grads(empty, grad_weight, full_grad, weight_rows, front)


def per_device(latents, cotangent, order, tstep, emb_table, gn_gain, weights):
    pipe_count = lax.axis_size("pipe")
    section_rank = lax.axis_index("pipe")
    mirror_rank = pipe_count - 1 - section_rank
    channels = latents.shape[2]
    places = latents.shape[3]
    slot_count = latents.shape[1]
    half_slots = slot_count // 2
    width = weights.shape[3]
    order_row = order[0]
    timestep_row = tstep[0]
    slot_ids = jnp.arange(slot_count, dtype=jnp.int32)
    picked = jnp.sum(
        jnp.where(order_row[:, None] == slot_ids[None, :], timestep_row[None, :], 0), axis=1
    )
    step_ids = jnp.arange(emb_table.shape[0], dtype=jnp.int32)
    one_hot = (picked[:, None] == step_ids[None, :]).astype(jnp.float32)
    entries_all = jnp.take(latents[0], order_row, axis=0)
    sections = (section_rank, mirror_rank)
    rows_list = []
    gains = []
    offsets_list = []
    inputs = []
    cotans = []
    for direction in range(2):
        section = sections[direction]
        rows_list.append(
            lax.dynamic_index_in_dim(weights, section, 0, keepdims=False).reshape(
                27 * channels, width
            )
        )
        gains.append(lax.dynamic_index_in_dim(gn_gain, section, 0, keepdims=False))
        table = lax.dynamic_index_in_dim(emb_table, section, 1, keepdims=False)
        hot_rows = one_hot[direction * half_slots : (direction + 1) * half_slots]
        offsets_list.append(jnp.dot(hot_rows, table, precision=lax.Precision.HIGHEST))
        inputs.append(entries_all[direction * half_slots : (direction + 1) * half_slots])
        cotans.append(cotangent[0, direction * half_slots : (direction + 1) * half_slots])
    ticks = pipe_count + half_slots - 1
    zero_field = jnp.zeros((channels, places), jnp.bfloat16)
    received = [zero_field, zero_field]
    stores = [jnp.zeros((half_slots, channels, places), jnp.bfloat16) for direction in range(2)]
    for tick_index in range(ticks):
        fronts = []
        entries_now = []
        lives = []
        for direction in range(2):
            section = sections[direction]
            micro = tick_index - section
            is_live = (micro >= 0) & (micro < half_slots)
            lives.append(is_live)
            clipped = jnp.clip(micro, 0, half_slots - 1)
            fresh = lax.dynamic_index_in_dim(inputs[direction], clipped, 0, keepdims=False)
            entry = jnp.where(section == 0, fresh, received[direction])
            kept = lax.dynamic_index_in_dim(stores[direction], clipped, 0, keepdims=False)
            stores[direction] = lax.dynamic_update_index_in_dim(
                stores[direction], jnp.where(is_live, entry, kept), clipped, 0
            )
            offset = lax.dynamic_index_in_dim(offsets_list[direction], clipped, 0, keepdims=False)
            active = pre_act(entry.astype(jnp.float32), gains[direction], offset).astype(
                jnp.bfloat16
            )
            fronts.append(tap_stack(active))
            entries_now.append(entry)
        if both_live(tick_index, pipe_count, half_slots, False):
            sums = conv_sums(rows_list, fronts)
        else:
            sums = conv_sum_single(rows_list, fronts, lives[0])
        results = [
            (entries_now[direction].astype(jnp.float32) + sums[direction]).astype(jnp.bfloat16)
            for direction in range(2)
        ]
        if tick_index + 1 < ticks:
            received = [passed_along(results[0], "pipe", 1), passed_along(results[1], "pipe", -1)]
    grads_in = [zero_field, zero_field]
    accums = [jnp.zeros((27 * channels, width), jnp.float32) for direction in range(2)]
    for tick_index in range(ticks):
        live_grads = []
        fronts = []
        pullers = []
        lives = []
        for direction in range(2):
            section = sections[direction]
            micro = tick_index - (pipe_count - 1 - section)
            is_live = (micro >= 0) & (micro < half_slots)
            lives.append(is_live)
            clipped = jnp.clip(micro, 0, half_slots - 1)
            fresh = lax.dynamic_index_in_dim(cotans[direction], clipped, 0, keepdims=False)
            incoming = jnp.where(section == pipe_count - 1, fresh, grads_in[direction])
            live_grads.append(jnp.where(is_live, incoming, zero_field))
            entry = lax.dynamic_index_in_dim(stores[direction], clipped, 0, keepdims=False)
            offset = lax.dynamic_index_in_dim(offsets_list[direction], clipped, 0, keepdims=False)
            active, pull = jax.vjp(
                partial(pre_act, gain=gains[direction], offset=offset), entry.astype(jnp.float32)
            )
            fronts.append(tap_stack(active.astype(jnp.bfloat16)))
            pullers.append(pull)
        if both_live(tick_index, pipe_count, half_slots, True):
            full_grads = gather_pair(live_grads)
        else:
            full_grads = gather_single(live_grads, lives)
        folded = [
            grad_fold(
                full_grads[direction], rows_list[direction], fronts[direction], accums[direction]
            )
            for direction in range(2)
        ]
        sends = []
        for direction in range(2):
            grad_taps, accums[direction] = folded[direction]
            back = pullers[direction](tap_adjoint(grad_taps, channels, places))[0]
            sends.append((live_grads[direction].astype(jnp.float32) + back).astype(jnp.bfloat16))
        if tick_index + 1 < ticks:
            grads_in = [passed_along(sends[0], "pipe", -1), passed_along(sends[1], "pipe", 1)]
    replica_count = lax.axis_size("dp")
    onward = ring_pairs(replica_count, pipe_count)
    backward_pairs = [(target, source) for source, target in onward]
    half = width // 2
    own, other = accums
    own_a, own_b = own[:, :half], own[:, half:]
    other_a, other_b = other[:, :half], other[:, half:]
    from_pred = ring_pass(jnp.concatenate([own_a, other_b], axis=1), onward)
    from_succ = ring_pass(jnp.concatenate([other_a, own_b], axis=1), backward_pairs)
    own_a = own_a + from_succ[:, :half]
    other_a = other_a + from_pred[:, :half]
    own_b = own_b + from_pred[:, half:]
    other_b = other_b + from_succ[:, half:]
    final_a = own_a + ring_pass(other_a, onward)
    final_b = own_b + ring_pass(other_b, backward_pairs)
    total = jnp.concatenate([final_a, final_b], axis=1)
    return total.reshape(1, 27, channels, width)


def solution(mesh):
    return jax.shard_map(
        per_device,
        mesh=mesh,
        in_specs=(
            P("dp", None, "chan", None),
            P("dp", None, "chan", None),
            P("dp", None),
            P("dp", None),
            P(None, None, "chan"),
            P(None, "chan"),
            P(None, None, "chan", None),
        ),
        out_specs=P("pipe", None, "chan", None),
        check_vma=False,
    )
```

```python
from functools import partial

import jax
import jax.numpy as jnp
from jax import lax
from jax.sharding import PartitionSpec as P

C = 640
GROUPS = 32
FR = 2
HT = 16
WD = 16


EPSILON = 1e-05


def passed_along(value, axis, steps):
    count = lax.axis_size(axis)
    first, last = (max(0, -steps), min(count, count - steps))
    return lax.ppermute(value, axis, [(source, source + steps) for source in range(first, last)])


def from_partner(value, axis, apart):
    mask = 2**apart
    pairs = [(source, source ^ mask) for source in range(lax.axis_size(axis))]
    return lax.ppermute(value, axis, pairs)


def ring_pairs(replica_count, pipe_count):
    pairs = []
    for replica in range(replica_count):
        for rank in range(pipe_count):
            step = 1 if rank >= pipe_count // 2 else 0
            target = ((replica + step) % replica_count) * pipe_count + pipe_count - 1 - rank
            pairs.append((replica * pipe_count + rank, target))
    return pairs


def ring_pass(value, pairs):
    moved = lax.ppermute(value.astype(jnp.bfloat16), ("dp", "pipe"), pairs)
    return moved.astype(jnp.float32)


def pre_act(field, gain, offset):
    channels, places = field.shape
    grouped = field.reshape(channels // (C // GROUPS), -1)
    centred = grouped - jnp.mean(grouped, axis=1, keepdims=True)
    spread = jnp.mean(centred * centred, axis=1, keepdims=True)
    normed = (centred * lax.rsqrt(spread + EPSILON)).reshape(channels, places)
    return jax.nn.silu(normed * gain[:, None] + offset[:, None])


def tap_stack(field):
    places = field.shape[1]
    plane = HT * WD
    margin = plane + WD + 1
    padded = jnp.pad(field, ((0, 0), (margin, margin)))
    position = jnp.arange(places, dtype=jnp.int32)
    frame_at = position // plane
    line_at = position // WD % HT
    column_at = position % WD
    pieces = []
    for shift_f in (-1, 0, 1):
        for shift_h in (-1, 0, 1):
            for shift_w in (-1, 0, 1):
                offset = shift_f * plane + shift_h * WD + shift_w
                inside = (frame_at + shift_f >= 0) & (frame_at + shift_f < FR)
                inside = inside & (line_at + shift_h >= 0) & (line_at + shift_h < HT)
                inside = inside & (column_at + shift_w >= 0) & (column_at + shift_w < WD)
                moved = lax.slice_in_dim(padded, margin + offset, margin + offset + places, axis=1)
                pieces.append(jnp.where(inside[None, :], moved, jnp.zeros_like(moved)))
    return jnp.concatenate(pieces, axis=0)


def tap_adjoint(grads, channels, places):
    pull = jax.vjp(tap_stack, jnp.zeros((channels, places), jnp.float32))[1]
    return pull(grads)[0]


def partial_term(weight_rows, front):
    return lax.dot_general(
        weight_rows, front, (((0,), (0,)), ((), ())), preferred_element_type=jnp.float32
    )


def conv_sums(rows_pair, fronts_pair):
    count = lax.axis_size("chan")
    parts = jnp.stack(
        [
            partial_term(rows, front).astype(jnp.bfloat16)
            for rows, front in zip(rows_pair, fronts_pair)
        ]
    )
    parts = parts.reshape(parts.shape[0], count, parts.shape[1] // count, parts.shape[2])
    got = lax.all_to_all(parts, "chan", 1, 1, tiled=False)
    sums = jnp.sum(got.astype(jnp.float32), axis=1)
    return [sums[direction] for direction in range(sums.shape[0])]


def conv_sum_single(rows_pair, fronts_pair, first_live):
    count = lax.axis_size("chan")
    first, second = [
        partial_term(rows, front).astype(jnp.bfloat16)
        for rows, front in zip(rows_pair, fronts_pair)
    ]
    part = jnp.where(first_live, first, second)
    part = part.reshape(count, part.shape[0] // count, part.shape[1])
    got = lax.all_to_all(part, "chan", 0, 0, tiled=False)
    total = jnp.sum(got.astype(jnp.float32), axis=0)
    return [total, total]


def gather_single(grads_pair, live_pair):
    count = lax.axis_size("chan")
    merged = grads_pair[0] + grads_pair[1]
    spread = jnp.broadcast_to(merged[None], (count,) + merged.shape)
    got = lax.all_to_all(spread, "chan", 0, 0, tiled=False)
    got = got.reshape(count * got.shape[1], got.shape[2])
    return [jnp.where(live, got, jnp.zeros_like(got)) for live in live_pair]


def both_live(tick_index, pipe_count, half_slots, backward):
    for rank in range(pipe_count):
        first = tick_index - (pipe_count - 1 - rank if backward else rank)
        second = tick_index - (rank if backward else pipe_count - 1 - rank)
        if 0 <= first < half_slots and 0 <= second < half_slots:
            return True
    return False


def gather_pair(grads_pair):
    count = lax.axis_size("chan")
    stacked = jnp.stack(grads_pair)
    spread = jnp.broadcast_to(stacked[:, None], (stacked.shape[0], count) + stacked.shape[1:])
    got = lax.all_to_all(spread, "chan", 1, 1, tiled=False)
    got = got.reshape(got.shape[0], count * got.shape[2], got.shape[3])
    return [got[direction] for direction in range(got.shape[0])]


def fold_grads(grad_taps, grad_weight, piece, weight_rows, front):
    grad_taps = jnp.dot(weight_rows, piece, preferred_element_type=jnp.float32)
    previous = grad_weight
    update = lax.dot_general(
        front, piece, (((1,), (1,)), ((), ())), preferred_element_type=jnp.float32
    )
    grad_weight = previous + update
    return (grad_taps, grad_weight)


def grad_fold(full_grad, weight_rows, front, grad_weight):
    empty = jnp.zeros(front.shape, jnp.float32)
    return fold_grads(empty, grad_weight, full_grad, weight_rows, front)


def per_device(latents, cotangent, order, tstep, emb_table, gn_gain, weights):
    pipe_count = lax.axis_size("pipe")
    section_rank = lax.axis_index("pipe")
    mirror_rank = pipe_count - 1 - section_rank
    channels = latents.shape[2]
    places = latents.shape[3]
    slot_count = latents.shape[1]
    half_slots = slot_count // 2
    width = weights.shape[3]
    order_row = order[0]
    timestep_row = tstep[0]
    slot_ids = jnp.arange(slot_count, dtype=jnp.int32)
    picked = jnp.sum(
        jnp.where(order_row[:, None] == slot_ids[None, :], timestep_row[None, :], 0), axis=1
    )
    step_ids = jnp.arange(emb_table.shape[0], dtype=jnp.int32)
    one_hot = (picked[:, None] == step_ids[None, :]).astype(jnp.float32)
    entries_all = jnp.take(latents[0], order_row, axis=0)
    sections = (section_rank, mirror_rank)
    rows_list = []
    gains = []
    offsets_list = []
    inputs = []
    cotans = []
    for direction in range(2):
        section = sections[direction]
        rows_list.append(
            lax.dynamic_index_in_dim(weights, section, 0, keepdims=False).reshape(
                27 * channels, width
            )
        )
        gains.append(lax.dynamic_index_in_dim(gn_gain, section, 0, keepdims=False))
        table = lax.dynamic_index_in_dim(emb_table, section, 1, keepdims=False)
        hot_rows = one_hot[direction * half_slots : (direction + 1) * half_slots]
        offsets_list.append(jnp.dot(hot_rows, table, precision=lax.Precision.HIGHEST))
        inputs.append(entries_all[direction * half_slots : (direction + 1) * half_slots])
        cotans.append(cotangent[0, direction * half_slots : (direction + 1) * half_slots])
    ticks = pipe_count + half_slots - 1
    zero_field = jnp.zeros((channels, places), jnp.bfloat16)
    received = [zero_field, zero_field]
    stores = [jnp.zeros((half_slots, channels, places), jnp.bfloat16) for direction in range(2)]
    for tick_index in range(ticks):
        fronts = []
        entries_now = []
        lives = []
        for direction in range(2):
            section = sections[direction]
            micro = tick_index - section
            is_live = (micro >= 0) & (micro < half_slots)
            lives.append(is_live)
            clipped = jnp.clip(micro, 0, half_slots - 1)
            fresh = lax.dynamic_index_in_dim(inputs[direction], clipped, 0, keepdims=False)
            entry = jnp.where(section == 0, fresh, received[direction])
            kept = lax.dynamic_index_in_dim(stores[direction], clipped, 0, keepdims=False)
            stores[direction] = lax.dynamic_update_index_in_dim(
                stores[direction], jnp.where(is_live, entry, kept), clipped, 0
            )
            offset = lax.dynamic_index_in_dim(offsets_list[direction], clipped, 0, keepdims=False)
            active = pre_act(entry.astype(jnp.float32), gains[direction], offset).astype(
                jnp.bfloat16
            )
            fronts.append(tap_stack(active))
            entries_now.append(entry)
        if both_live(tick_index, pipe_count, half_slots, False):
            sums = conv_sums(rows_list, fronts)
        else:
            sums = conv_sum_single(rows_list, fronts, lives[0])
        results = [
            (entries_now[direction].astype(jnp.float32) + sums[direction]).astype(jnp.bfloat16)
            for direction in range(2)
        ]
        if tick_index + 1 < ticks:
            received = [passed_along(results[0], "pipe", 1), passed_along(results[1], "pipe", -1)]
    grads_in = [zero_field, zero_field]
    accums = [jnp.zeros((27 * channels, width), jnp.float32) for direction in range(2)]
    for tick_index in range(ticks):
        live_grads = []
        fronts = []
        pullers = []
        lives = []
        for direction in range(2):
            section = sections[direction]
            micro = tick_index - (pipe_count - 1 - section)
            is_live = (micro >= 0) & (micro < half_slots)
            lives.append(is_live)
            clipped = jnp.clip(micro, 0, half_slots - 1)
            fresh = lax.dynamic_index_in_dim(cotans[direction], clipped, 0, keepdims=False)
            incoming = jnp.where(section == pipe_count - 1, fresh, grads_in[direction])
            live_grads.append(jnp.where(is_live, incoming, zero_field))
            entry = lax.dynamic_index_in_dim(stores[direction], clipped, 0, keepdims=False)
            offset = lax.dynamic_index_in_dim(offsets_list[direction], clipped, 0, keepdims=False)
            active, pull = jax.vjp(
                partial(pre_act, gain=gains[direction], offset=offset), entry.astype(jnp.float32)
            )
            fronts.append(tap_stack(active.astype(jnp.bfloat16)))
            pullers.append(pull)
        if both_live(tick_index, pipe_count, half_slots, True):
            full_grads = gather_pair(live_grads)
        else:
            full_grads = gather_single(live_grads, lives)
        folded = [
            grad_fold(
                full_grads[direction], rows_list[direction], fronts[direction], accums[direction]
            )
            for direction in range(2)
        ]
        sends = []
        for direction in range(2):
            grad_taps, accums[direction] = folded[direction]
            back = pullers[direction](tap_adjoint(grad_taps, channels, places))[0]
            sends.append((live_grads[direction].astype(jnp.float32) + back).astype(jnp.bfloat16))
        if tick_index + 1 < ticks:
            grads_in = [passed_along(sends[0], "pipe", -1), passed_along(sends[1], "pipe", 1)]
    replica_count = lax.axis_size("dp")
    onward = ring_pairs(replica_count, pipe_count)
    backward_pairs = [(target, source) for source, target in onward]
    taps = accums[0].shape[0] // channels
    half = (taps + 1) // 2
    own, other = [accum.reshape(taps, channels, width) for accum in accums]
    own_a, own_b = own[:half], own[half:]
    other_a, other_b = other[:half], other[half:]
    from_pred = ring_pass(jnp.concatenate([own_a, other_b], axis=0), onward)
    from_succ = ring_pass(jnp.concatenate([other_a, own_b], axis=0), backward_pairs)
    own_a = own_a + from_succ[:half]
    other_a = other_a + from_pred[:half]
    own_b = own_b + from_pred[half:]
    other_b = other_b + from_succ[half:]
    final_a = own_a + ring_pass(other_a, onward)
    final_b = own_b + ring_pass(other_b, backward_pairs)
    total = jnp.concatenate([final_a, final_b], axis=0)
    return total.reshape(1, 27, channels, width)


def solution(mesh):
    return jax.shard_map(
        per_device,
        mesh=mesh,
        in_specs=(
            P("dp", None, "chan", None),
            P("dp", None, "chan", None),
            P("dp", None),
            P("dp", None),
            P(None, None, "chan"),
            P(None, "chan"),
            P(None, None, "chan", None),
        ),
        out_specs=P("pipe", None, "chan", None),
        check_vma=False,
    )
```

```python
from functools import partial

import jax
import jax.numpy as jnp
from jax import lax
from jax.sharding import PartitionSpec as P

C = 640
GROUPS = 32
FR = 2
HT = 16
WD = 16


EPSILON = 1e-05


def passed_along(value, axis, steps):
    count = lax.axis_size(axis)
    first, last = (max(0, -steps), min(count, count - steps))
    return lax.ppermute(value, axis, [(source, source + steps) for source in range(first, last)])


def from_partner(value, axis, apart):
    mask = 2**apart
    pairs = [(source, source ^ mask) for source in range(lax.axis_size(axis))]
    return lax.ppermute(value, axis, pairs)


def ring_pairs(replica_count, pipe_count):
    pairs = []
    for replica in range(replica_count):
        for rank in range(pipe_count):
            step = 1 if rank >= pipe_count // 2 else 0
            target = ((replica + step) % replica_count) * pipe_count + pipe_count - 1 - rank
            pairs.append((replica * pipe_count + rank, target))
    return pairs


def ring_pass(value, pairs):
    moved = lax.ppermute(value.astype(jnp.bfloat16), ("dp", "pipe"), pairs)
    return moved.astype(jnp.float32)


def pre_act(field, gain, offset):
    channels, places = field.shape
    grouped = field.reshape(channels // (C // GROUPS), -1)
    centred = grouped - jnp.mean(grouped, axis=1, keepdims=True)
    spread = jnp.mean(centred * centred, axis=1, keepdims=True)
    normed = (centred * lax.rsqrt(spread + EPSILON)).reshape(channels, places)
    return jax.nn.silu(normed * gain[:, None] + offset[:, None])


def tap_stack(field):
    places = field.shape[1]
    plane = HT * WD
    margin = plane + WD + 1
    padded = jnp.pad(field, ((0, 0), (margin, margin)))
    position = jnp.arange(places, dtype=jnp.int32)
    frame_at = position // plane
    line_at = position // WD % HT
    column_at = position % WD
    pieces = []
    for shift_f in (-1, 0, 1):
        for shift_h in (-1, 0, 1):
            for shift_w in (-1, 0, 1):
                offset = shift_f * plane + shift_h * WD + shift_w
                inside = (frame_at + shift_f >= 0) & (frame_at + shift_f < FR)
                inside = inside & (line_at + shift_h >= 0) & (line_at + shift_h < HT)
                inside = inside & (column_at + shift_w >= 0) & (column_at + shift_w < WD)
                moved = lax.slice_in_dim(padded, margin + offset, margin + offset + places, axis=1)
                pieces.append(jnp.where(inside[None, :], moved, jnp.zeros_like(moved)))
    return jnp.concatenate(pieces, axis=0)


def tap_adjoint(grads, channels, places):
    pull = jax.vjp(tap_stack, jnp.zeros((channels, places), jnp.float32))[1]
    return pull(grads)[0]


def partial_term(weight_rows, front):
    return lax.dot_general(
        weight_rows, front, (((0,), (0,)), ((), ())), preferred_element_type=jnp.float32
    )


def conv_sums(rows_pair, fronts_pair):
    count = lax.axis_size("chan")
    parts = jnp.stack(
        [
            partial_term(rows, front).astype(jnp.bfloat16)
            for rows, front in zip(rows_pair, fronts_pair)
        ]
    )
    parts = parts.reshape(parts.shape[0], count, parts.shape[1] // count, parts.shape[2])
    got = lax.all_to_all(parts, "chan", 1, 1, tiled=False)
    sums = jnp.sum(got.astype(jnp.float32), axis=1)
    return [sums[direction] for direction in range(sums.shape[0])]


def conv_sum_single(rows_pair, fronts_pair, first_live):
    count = lax.axis_size("chan")
    first, second = [
        partial_term(rows, front).astype(jnp.bfloat16)
        for rows, front in zip(rows_pair, fronts_pair)
    ]
    part = jnp.where(first_live, first, second)
    part = part.reshape(count, part.shape[0] // count, part.shape[1])
    got = lax.all_to_all(part, "chan", 0, 0, tiled=False)
    total = jnp.sum(got.astype(jnp.float32), axis=0)
    return [total, total]


def gather_single(grads_pair, live_pair):
    count = lax.axis_size("chan")
    merged = grads_pair[0] + grads_pair[1]
    spread = jnp.broadcast_to(merged[None], (count,) + merged.shape)
    got = lax.all_to_all(spread, "chan", 0, 0, tiled=False)
    got = got.reshape(count * got.shape[1], got.shape[2])
    return [jnp.where(live, got, jnp.zeros_like(got)) for live in live_pair]


def both_live(tick_index, pipe_count, half_slots, backward):
    for rank in range(pipe_count):
        first = tick_index - (pipe_count - 1 - rank if backward else rank)
        second = tick_index - (rank if backward else pipe_count - 1 - rank)
        if 0 <= first < half_slots and 0 <= second < half_slots:
            return True
    return False


def conv_one(rows, front):
    count = lax.axis_size("chan")
    part = partial_term(rows, front).astype(jnp.bfloat16)
    part = part.reshape(count, part.shape[0] // count, part.shape[1])
    got = lax.all_to_all(part, "chan", 0, 0, tiled=False)
    return jnp.sum(got.astype(jnp.float32), axis=0)


def gather_one(grad):
    count = lax.axis_size("chan")
    spread = jnp.broadcast_to(grad[None], (count,) + grad.shape)
    got = lax.all_to_all(spread, "chan", 0, 0, tiled=False)
    return got.reshape(count * got.shape[1], got.shape[2])


def gather_pair(grads_pair):
    count = lax.axis_size("chan")
    stacked = jnp.stack(grads_pair)
    spread = jnp.broadcast_to(stacked[:, None], (stacked.shape[0], count) + stacked.shape[1:])
    got = lax.all_to_all(spread, "chan", 1, 1, tiled=False)
    got = got.reshape(got.shape[0], count * got.shape[2], got.shape[3])
    return [got[direction] for direction in range(got.shape[0])]


def fold_grads(grad_taps, grad_weight, piece, weight_rows, front):
    grad_taps = jnp.dot(weight_rows, piece, preferred_element_type=jnp.float32)
    previous = grad_weight
    update = lax.dot_general(
        front, piece, (((1,), (1,)), ((), ())), preferred_element_type=jnp.float32
    )
    grad_weight = previous + update
    return (grad_taps, grad_weight)


def grad_fold(full_grad, weight_rows, front, grad_weight):
    empty = jnp.zeros(front.shape, jnp.float32)
    return fold_grads(empty, grad_weight, full_grad, weight_rows, front)


def per_device(latents, cotangent, order, tstep, emb_table, gn_gain, weights):
    pipe_count = lax.axis_size("pipe")
    section_rank = lax.axis_index("pipe")
    mirror_rank = pipe_count - 1 - section_rank
    channels = latents.shape[2]
    places = latents.shape[3]
    slot_count = latents.shape[1]
    half_slots = slot_count // 2
    width = weights.shape[3]
    order_row = order[0]
    timestep_row = tstep[0]
    slot_ids = jnp.arange(slot_count, dtype=jnp.int32)
    picked = jnp.sum(
        jnp.where(order_row[:, None] == slot_ids[None, :], timestep_row[None, :], 0), axis=1
    )
    step_ids = jnp.arange(emb_table.shape[0], dtype=jnp.int32)
    one_hot = (picked[:, None] == step_ids[None, :]).astype(jnp.float32)
    entries_all = jnp.take(latents[0], order_row, axis=0)
    sections = (section_rank, mirror_rank)
    rows_list = []
    gains = []
    offsets_list = []
    inputs = []
    cotans = []
    for direction in range(2):
        section = sections[direction]
        rows_list.append(
            lax.dynamic_index_in_dim(weights, section, 0, keepdims=False).reshape(
                27 * channels, width
            )
        )
        gains.append(lax.dynamic_index_in_dim(gn_gain, section, 0, keepdims=False))
        table = lax.dynamic_index_in_dim(emb_table, section, 1, keepdims=False)
        hot_rows = one_hot[direction * half_slots : (direction + 1) * half_slots]
        offsets_list.append(jnp.dot(hot_rows, table, precision=lax.Precision.HIGHEST))
        inputs.append(entries_all[direction * half_slots : (direction + 1) * half_slots])
        cotans.append(cotangent[0, direction * half_slots : (direction + 1) * half_slots])
    ticks = pipe_count + half_slots - 1
    zero_field = jnp.zeros((channels, places), jnp.bfloat16)
    received = [zero_field, zero_field]
    stores = [jnp.zeros((half_slots, channels, places), jnp.bfloat16) for direction in range(2)]
    rows_stack = jnp.stack(rows_list)
    for tick_index in range(ticks):
        entries_now = []
        offsets_now = []
        lives = []
        for direction in range(2):
            section = sections[direction]
            micro = tick_index - section
            is_live = (micro >= 0) & (micro < half_slots)
            lives.append(is_live)
            clipped = jnp.clip(micro, 0, half_slots - 1)
            fresh = lax.dynamic_index_in_dim(inputs[direction], clipped, 0, keepdims=False)
            entry = jnp.where(section == 0, fresh, received[direction])
            kept = lax.dynamic_index_in_dim(stores[direction], clipped, 0, keepdims=False)
            stores[direction] = lax.dynamic_update_index_in_dim(
                stores[direction], jnp.where(is_live, entry, kept), clipped, 0
            )
            offsets_now.append(
                lax.dynamic_index_in_dim(offsets_list[direction], clipped, 0, keepdims=False)
            )
            entries_now.append(entry)
        if both_live(tick_index, pipe_count, half_slots, False):
            fronts = [
                tap_stack(
                    pre_act(
                        entries_now[direction].astype(jnp.float32),
                        gains[direction],
                        offsets_now[direction],
                    ).astype(jnp.bfloat16)
                )
                for direction in range(2)
            ]
            sums = conv_sums(rows_list, fronts)
        else:
            pick = lives[0]
            entry = jnp.where(pick, entries_now[0], entries_now[1])
            gain = jnp.where(pick, gains[0], gains[1])
            offset = jnp.where(pick, offsets_now[0], offsets_now[1])
            rows = lax.dynamic_index_in_dim(rows_stack, jnp.where(pick, 0, 1), 0, keepdims=False)
            front = tap_stack(pre_act(entry.astype(jnp.float32), gain, offset).astype(jnp.bfloat16))
            total = conv_one(rows, front)
            sums = [total, total]
        results = [
            (entries_now[direction].astype(jnp.float32) + sums[direction]).astype(jnp.bfloat16)
            for direction in range(2)
        ]
        if tick_index + 1 < ticks:
            received = [passed_along(results[0], "pipe", 1), passed_along(results[1], "pipe", -1)]
    grads_in = [zero_field, zero_field]
    acc_stack = jnp.zeros((2, 27 * channels, width), jnp.float32)
    for tick_index in range(ticks):
        live_grads = []
        entries_now = []
        offsets_now = []
        lives = []
        for direction in range(2):
            section = sections[direction]
            micro = tick_index - (pipe_count - 1 - section)
            is_live = (micro >= 0) & (micro < half_slots)
            lives.append(is_live)
            clipped = jnp.clip(micro, 0, half_slots - 1)
            fresh = lax.dynamic_index_in_dim(cotans[direction], clipped, 0, keepdims=False)
            incoming = jnp.where(section == pipe_count - 1, fresh, grads_in[direction])
            live_grads.append(jnp.where(is_live, incoming, zero_field))
            entries_now.append(lax.dynamic_index_in_dim(stores[direction], clipped, 0, keepdims=False))
            offsets_now.append(
                lax.dynamic_index_in_dim(offsets_list[direction], clipped, 0, keepdims=False)
            )
        sends = []
        if both_live(tick_index, pipe_count, half_slots, True):
            full_grads = gather_pair(live_grads)
            for direction in range(2):
                active, pull = jax.vjp(
                    partial(pre_act, gain=gains[direction], offset=offsets_now[direction]),
                    entries_now[direction].astype(jnp.float32),
                )
                front = tap_stack(active.astype(jnp.bfloat16))
                grad_taps, update = fold_grads(
                    None, 0.0, full_grads[direction], rows_list[direction], front
                )
                acc_stack = acc_stack.at[direction].add(update)
                back = pull(tap_adjoint(grad_taps, channels, places))[0]
                sends.append(
                    (live_grads[direction].astype(jnp.float32) + back).astype(jnp.bfloat16)
                )
        else:
            pick = lives[0]
            chosen = jnp.where(pick, 0, 1)
            entry = jnp.where(pick, entries_now[0], entries_now[1])
            gain = jnp.where(pick, gains[0], gains[1])
            offset = jnp.where(pick, offsets_now[0], offsets_now[1])
            active, pull = jax.vjp(partial(pre_act, gain=gain, offset=offset), entry.astype(jnp.float32))
            front = tap_stack(active.astype(jnp.bfloat16))
            full = gather_one(live_grads[0] + live_grads[1])
            rows = lax.dynamic_index_in_dim(rows_stack, chosen, 0, keepdims=False)
            grad_taps, update = fold_grads(None, 0.0, full, rows, front)
            previous = lax.dynamic_index_in_dim(acc_stack, chosen, 0, keepdims=False)
            acc_stack = lax.dynamic_update_index_in_dim(acc_stack, previous + update, chosen, 0)
            back = pull(tap_adjoint(grad_taps, channels, places))[0]
            for direction in range(2):
                sends.append(
                    (live_grads[direction].astype(jnp.float32) + back).astype(jnp.bfloat16)
                )
        if tick_index + 1 < ticks:
            grads_in = [passed_along(sends[0], "pipe", -1), passed_along(sends[1], "pipe", 1)]
    accums = [acc_stack[0], acc_stack[1]]
    replica_count = lax.axis_size("dp")
    onward = ring_pairs(replica_count, pipe_count)
    backward_pairs = [(target, source) for source, target in onward]
    taps = accums[0].shape[0] // channels
    half = (taps + 1) // 2
    own, other = [accum.reshape(taps, channels, width) for accum in accums]
    own_a, own_b = own[:half], own[half:]
    other_a, other_b = other[:half], other[half:]
    from_pred = ring_pass(jnp.concatenate([own_a, other_b], axis=0), onward)
    from_succ = ring_pass(jnp.concatenate([other_a, own_b], axis=0), backward_pairs)
    own_a = own_a + from_succ[:half]
    other_a = other_a + from_pred[:half]
    own_b = own_b + from_pred[half:]
    other_b = other_b + from_succ[half:]
    final_a = own_a + ring_pass(other_a, onward)
    final_b = own_b + ring_pass(other_b, backward_pairs)
    total = jnp.concatenate([final_a, final_b], axis=0)
    return total.reshape(1, 27, channels, width)


def solution(mesh):
    return jax.shard_map(
        per_device,
        mesh=mesh,
        in_specs=(
            P("dp", None, "chan", None),
            P("dp", None, "chan", None),
            P("dp", None),
            P("dp", None),
            P(None, None, "chan"),
            P(None, "chan"),
            P(None, None, "chan", None),
        ),
        out_specs=P("pipe", None, "chan", None),
        check_vma=False,
    )
```

```python
from functools import partial

import jax
import jax.numpy as jnp
from jax import lax
from jax.sharding import PartitionSpec as P

C = 640
GROUPS = 32
FR = 2
HT = 16
WD = 16


EPSILON = 1e-05


def passed_along(value, axis, steps):
    count = lax.axis_size(axis)
    first, last = (max(0, -steps), min(count, count - steps))
    return lax.ppermute(value, axis, [(source, source + steps) for source in range(first, last)])


def from_partner(value, axis, apart):
    mask = 2**apart
    pairs = [(source, source ^ mask) for source in range(lax.axis_size(axis))]
    return lax.ppermute(value, axis, pairs)


def ring_pairs(replica_count, pipe_count):
    pairs = []
    for replica in range(replica_count):
        for rank in range(pipe_count):
            step = 1 if rank >= pipe_count // 2 else 0
            target = ((replica + step) % replica_count) * pipe_count + pipe_count - 1 - rank
            pairs.append((replica * pipe_count + rank, target))
    return pairs


def ring_pass(value, pairs):
    moved = lax.ppermute(value.astype(jnp.bfloat16), ("dp", "pipe"), pairs)
    return moved.astype(jnp.float32)


def pre_act(field, gain, offset):
    channels, places = field.shape
    grouped = field.reshape(channels // (C // GROUPS), -1)
    centred = grouped - jnp.mean(grouped, axis=1, keepdims=True)
    spread = jnp.mean(centred * centred, axis=1, keepdims=True)
    normed = (centred * lax.rsqrt(spread + EPSILON)).reshape(channels, places)
    return jax.nn.silu(normed * gain[:, None] + offset[:, None])


def tap_stack(field):
    places = field.shape[1]
    plane = HT * WD
    margin = plane + WD + 1
    padded = jnp.pad(field, ((0, 0), (margin, margin)))
    position = jnp.arange(places, dtype=jnp.int32)
    frame_at = position // plane
    line_at = position // WD % HT
    column_at = position % WD
    pieces = []
    for shift_f in (-1, 0, 1):
        for shift_h in (-1, 0, 1):
            for shift_w in (-1, 0, 1):
                offset = shift_f * plane + shift_h * WD + shift_w
                inside = (frame_at + shift_f >= 0) & (frame_at + shift_f < FR)
                inside = inside & (line_at + shift_h >= 0) & (line_at + shift_h < HT)
                inside = inside & (column_at + shift_w >= 0) & (column_at + shift_w < WD)
                moved = lax.slice_in_dim(padded, margin + offset, margin + offset + places, axis=1)
                pieces.append(jnp.where(inside[None, :], moved, jnp.zeros_like(moved)))
    return jnp.concatenate(pieces, axis=0)


def tap_adjoint(grads, channels, places):
    pull = jax.vjp(tap_stack, jnp.zeros((channels, places), jnp.float32))[1]
    return pull(grads)[0]


def partial_term(weight_rows, front):
    return lax.dot_general(
        weight_rows, front, (((0,), (0,)), ((), ())), preferred_element_type=jnp.float32
    )


def conv_sums(rows_pair, fronts_pair):
    count = lax.axis_size("chan")
    parts = jnp.stack(
        [
            partial_term(rows, front).astype(jnp.bfloat16)
            for rows, front in zip(rows_pair, fronts_pair)
        ]
    )
    parts = parts.reshape(parts.shape[0], count, parts.shape[1] // count, parts.shape[2])
    got = lax.all_to_all(parts, "chan", 1, 1, tiled=False)
    sums = jnp.sum(got.astype(jnp.float32), axis=1)
    return [sums[direction] for direction in range(sums.shape[0])]


def conv_sum_single(rows_pair, fronts_pair, first_live):
    count = lax.axis_size("chan")
    first, second = [
        partial_term(rows, front).astype(jnp.bfloat16)
        for rows, front in zip(rows_pair, fronts_pair)
    ]
    part = jnp.where(first_live, first, second)
    part = part.reshape(count, part.shape[0] // count, part.shape[1])
    got = lax.all_to_all(part, "chan", 0, 0, tiled=False)
    total = jnp.sum(got.astype(jnp.float32), axis=0)
    return [total, total]


def gather_single(grads_pair, live_pair):
    count = lax.axis_size("chan")
    merged = grads_pair[0] + grads_pair[1]
    spread = jnp.broadcast_to(merged[None], (count,) + merged.shape)
    got = lax.all_to_all(spread, "chan", 0, 0, tiled=False)
    got = got.reshape(count * got.shape[1], got.shape[2])
    return [jnp.where(live, got, jnp.zeros_like(got)) for live in live_pair]


def live_at(tick_index, rank, direction, pipe_count, half_slots, backward):
    section = rank if direction == 0 else pipe_count - 1 - rank
    lag = pipe_count - 1 - section if backward else section
    return 0 <= tick_index - lag < half_slots


def relay(values, tick_index, pipe_count, half_slots, backward):
    pair_lists = []
    for direction in range(2):
        step = (1 if direction == 0 else -1) * (-1 if backward else 1)
        pairs = []
        for rank in range(pipe_count):
            target = rank + step
            if 0 <= target < pipe_count and live_at(
                tick_index, rank, direction, pipe_count, half_slots, backward
            ):
                pairs.append((rank, target))
        pair_lists.append(pairs)
    union = pair_lists[0] + pair_lists[1]
    sources = [source for source, _ in union]
    targets = [target for _, target in union]
    if len(set(sources)) == len(union) and len(set(targets)) == len(union):
        if not union:
            return [jnp.zeros_like(values[0]), jnp.zeros_like(values[1])]
        first_sources = jnp.array([source for source, _ in pair_lists[0]] + [-1], jnp.int32)
        rank_now = lax.axis_index("pipe")
        picked = jnp.where(jnp.any(first_sources == rank_now), values[0], values[1])
        got = lax.ppermute(picked, "pipe", union)
        return [got, got]
    moved = []
    for direction in range(2):
        if pair_lists[direction]:
            moved.append(lax.ppermute(values[direction], "pipe", pair_lists[direction]))
        else:
            moved.append(jnp.zeros_like(values[direction]))
    return moved


def both_live(tick_index, pipe_count, half_slots, backward):
    for rank in range(pipe_count):
        first = tick_index - (pipe_count - 1 - rank if backward else rank)
        second = tick_index - (rank if backward else pipe_count - 1 - rank)
        if 0 <= first < half_slots and 0 <= second < half_slots:
            return True
    return False


def conv_one(rows, front):
    count = lax.axis_size("chan")
    part = partial_term(rows, front).astype(jnp.bfloat16)
    part = part.reshape(count, part.shape[0] // count, part.shape[1])
    got = lax.all_to_all(part, "chan", 0, 0, tiled=False)
    return jnp.sum(got.astype(jnp.float32), axis=0)


def gather_one(grad):
    count = lax.axis_size("chan")
    spread = jnp.broadcast_to(grad[None], (count,) + grad.shape)
    got = lax.all_to_all(spread, "chan", 0, 0, tiled=False)
    return got.reshape(count * got.shape[1], got.shape[2])


def gather_pair(grads_pair):
    count = lax.axis_size("chan")
    stacked = jnp.stack(grads_pair)
    spread = jnp.broadcast_to(stacked[:, None], (stacked.shape[0], count) + stacked.shape[1:])
    got = lax.all_to_all(spread, "chan", 1, 1, tiled=False)
    got = got.reshape(got.shape[0], count * got.shape[2], got.shape[3])
    return [got[direction] for direction in range(got.shape[0])]


def fold_grads(grad_taps, grad_weight, piece, weight_rows, front):
    grad_taps = jnp.dot(weight_rows, piece, preferred_element_type=jnp.float32)
    previous = grad_weight
    update = lax.dot_general(
        front, piece, (((1,), (1,)), ((), ())), preferred_element_type=jnp.float32
    )
    grad_weight = previous + update
    return (grad_taps, grad_weight)


def grad_fold(full_grad, weight_rows, front, grad_weight):
    empty = jnp.zeros(front.shape, jnp.float32)
    return fold_grads(empty, grad_weight, full_grad, weight_rows, front)


def per_device(latents, cotangent, order, tstep, emb_table, gn_gain, weights):
    pipe_count = lax.axis_size("pipe")
    section_rank = lax.axis_index("pipe")
    mirror_rank = pipe_count - 1 - section_rank
    channels = latents.shape[2]
    places = latents.shape[3]
    slot_count = latents.shape[1]
    half_slots = slot_count // 2
    width = weights.shape[3]
    order_row = order[0]
    timestep_row = tstep[0]
    slot_ids = jnp.arange(slot_count, dtype=jnp.int32)
    picked = jnp.sum(
        jnp.where(order_row[:, None] == slot_ids[None, :], timestep_row[None, :], 0), axis=1
    )
    step_ids = jnp.arange(emb_table.shape[0], dtype=jnp.int32)
    one_hot = (picked[:, None] == step_ids[None, :]).astype(jnp.float32)
    entries_all = jnp.take(latents[0], order_row, axis=0)
    sections = (section_rank, mirror_rank)
    rows_list = []
    gains = []
    offsets_list = []
    inputs = []
    cotans = []
    for direction in range(2):
        section = sections[direction]
        rows_list.append(
            lax.dynamic_index_in_dim(weights, section, 0, keepdims=False).reshape(
                27 * channels, width
            )
        )
        gains.append(lax.dynamic_index_in_dim(gn_gain, section, 0, keepdims=False))
        table = lax.dynamic_index_in_dim(emb_table, section, 1, keepdims=False)
        hot_rows = one_hot[direction * half_slots : (direction + 1) * half_slots]
        offsets_list.append(jnp.dot(hot_rows, table, precision=lax.Precision.HIGHEST))
        inputs.append(entries_all[direction * half_slots : (direction + 1) * half_slots])
        cotans.append(cotangent[0, direction * half_slots : (direction + 1) * half_slots])
    ticks = pipe_count + half_slots - 1
    zero_field = jnp.zeros((channels, places), jnp.bfloat16)
    received = [zero_field, zero_field]
    stores = [jnp.zeros((half_slots, channels, places), jnp.bfloat16) for direction in range(2)]
    rows_stack = jnp.stack(rows_list)
    for tick_index in range(ticks):
        entries_now = []
        offsets_now = []
        lives = []
        for direction in range(2):
            section = sections[direction]
            micro = tick_index - section
            is_live = (micro >= 0) & (micro < half_slots)
            lives.append(is_live)
            clipped = jnp.clip(micro, 0, half_slots - 1)
            fresh = lax.dynamic_index_in_dim(inputs[direction], clipped, 0, keepdims=False)
            entry = jnp.where(section == 0, fresh, received[direction])
            kept = lax.dynamic_index_in_dim(stores[direction], clipped, 0, keepdims=False)
            stores[direction] = lax.dynamic_update_index_in_dim(
                stores[direction], jnp.where(is_live, entry, kept), clipped, 0
            )
            offsets_now.append(
                lax.dynamic_index_in_dim(offsets_list[direction], clipped, 0, keepdims=False)
            )
            entries_now.append(entry)
        if both_live(tick_index, pipe_count, half_slots, False):
            fronts = [
                tap_stack(
                    pre_act(
                        entries_now[direction].astype(jnp.float32),
                        gains[direction],
                        offsets_now[direction],
                    ).astype(jnp.bfloat16)
                )
                for direction in range(2)
            ]
            sums = conv_sums(rows_list, fronts)
        else:
            pick = lives[0]
            entry = jnp.where(pick, entries_now[0], entries_now[1])
            gain = jnp.where(pick, gains[0], gains[1])
            offset = jnp.where(pick, offsets_now[0], offsets_now[1])
            rows = lax.dynamic_index_in_dim(rows_stack, jnp.where(pick, 0, 1), 0, keepdims=False)
            front = tap_stack(pre_act(entry.astype(jnp.float32), gain, offset).astype(jnp.bfloat16))
            total = conv_one(rows, front)
            sums = [total, total]
        results = [
            (entries_now[direction].astype(jnp.float32) + sums[direction]).astype(jnp.bfloat16)
            for direction in range(2)
        ]
        if tick_index + 1 < ticks:
            received = relay(results, tick_index, pipe_count, half_slots, False)
    grads_in = [zero_field, zero_field]
    acc_stack = jnp.zeros((2, 27 * channels, width), jnp.float32)
    for tick_index in range(ticks):
        live_grads = []
        entries_now = []
        offsets_now = []
        lives = []
        for direction in range(2):
            section = sections[direction]
            micro = tick_index - (pipe_count - 1 - section)
            is_live = (micro >= 0) & (micro < half_slots)
            lives.append(is_live)
            clipped = jnp.clip(micro, 0, half_slots - 1)
            fresh = lax.dynamic_index_in_dim(cotans[direction], clipped, 0, keepdims=False)
            incoming = jnp.where(section == pipe_count - 1, fresh, grads_in[direction])
            live_grads.append(jnp.where(is_live, incoming, zero_field))
            entries_now.append(lax.dynamic_index_in_dim(stores[direction], clipped, 0, keepdims=False))
            offsets_now.append(
                lax.dynamic_index_in_dim(offsets_list[direction], clipped, 0, keepdims=False)
            )
        sends = []
        if both_live(tick_index, pipe_count, half_slots, True):
            full_grads = gather_pair(live_grads)
            for direction in range(2):
                active, pull = jax.vjp(
                    partial(pre_act, gain=gains[direction], offset=offsets_now[direction]),
                    entries_now[direction].astype(jnp.float32),
                )
                front = tap_stack(active.astype(jnp.bfloat16))
                grad_taps, update = fold_grads(
                    None, 0.0, full_grads[direction], rows_list[direction], front
                )
                acc_stack = acc_stack.at[direction].add(update)
                back = pull(tap_adjoint(grad_taps, channels, places))[0]
                sends.append(
                    (live_grads[direction].astype(jnp.float32) + back).astype(jnp.bfloat16)
                )
        else:
            pick = lives[0]
            chosen = jnp.where(pick, 0, 1)
            entry = jnp.where(pick, entries_now[0], entries_now[1])
            gain = jnp.where(pick, gains[0], gains[1])
            offset = jnp.where(pick, offsets_now[0], offsets_now[1])
            active, pull = jax.vjp(partial(pre_act, gain=gain, offset=offset), entry.astype(jnp.float32))
            front = tap_stack(active.astype(jnp.bfloat16))
            full = gather_one(live_grads[0] + live_grads[1])
            rows = lax.dynamic_index_in_dim(rows_stack, chosen, 0, keepdims=False)
            grad_taps, update = fold_grads(None, 0.0, full, rows, front)
            previous = lax.dynamic_index_in_dim(acc_stack, chosen, 0, keepdims=False)
            acc_stack = lax.dynamic_update_index_in_dim(acc_stack, previous + update, chosen, 0)
            back = pull(tap_adjoint(grad_taps, channels, places))[0]
            for direction in range(2):
                sends.append(
                    (live_grads[direction].astype(jnp.float32) + back).astype(jnp.bfloat16)
                )
        if tick_index + 1 < ticks:
            grads_in = relay(sends, tick_index, pipe_count, half_slots, True)
    accums = [acc_stack[0], acc_stack[1]]
    replica_count = lax.axis_size("dp")
    onward = ring_pairs(replica_count, pipe_count)
    backward_pairs = [(target, source) for source, target in onward]
    taps = accums[0].shape[0] // channels
    half = (taps + 1) // 2
    own, other = [accum.reshape(taps, channels, width) for accum in accums]
    own_a, own_b = own[:half], own[half:]
    other_a, other_b = other[:half], other[half:]
    from_pred = ring_pass(jnp.concatenate([own_a, other_b], axis=0), onward)
    from_succ = ring_pass(jnp.concatenate([other_a, own_b], axis=0), backward_pairs)
    own_a = own_a + from_succ[:half]
    other_a = other_a + from_pred[:half]
    own_b = own_b + from_pred[half:]
    other_b = other_b + from_succ[half:]
    final_a = own_a + ring_pass(other_a, onward)
    final_b = own_b + ring_pass(other_b, backward_pairs)
    total = jnp.concatenate([final_a, final_b], axis=0)
    return total.reshape(1, 27, channels, width)


def solution(mesh):
    return jax.shard_map(
        per_device,
        mesh=mesh,
        in_specs=(
            P("dp", None, "chan", None),
            P("dp", None, "chan", None),
            P("dp", None),
            P("dp", None),
            P(None, None, "chan"),
            P(None, "chan"),
            P(None, None, "chan", None),
        ),
        out_specs=P("pipe", None, "chan", None),
        check_vma=False,
    )
```

```python
from functools import partial

import jax
import jax.numpy as jnp
from jax import lax
from jax.sharding import PartitionSpec as P

C = 640
GROUPS = 32
FR = 2
HT = 16
WD = 16


EPSILON = 1e-05


def passed_along(value, axis, steps):
    count = lax.axis_size(axis)
    first, last = (max(0, -steps), min(count, count - steps))
    return lax.ppermute(value, axis, [(source, source + steps) for source in range(first, last)])


def from_partner(value, axis, apart):
    mask = 2**apart
    pairs = [(source, source ^ mask) for source in range(lax.axis_size(axis))]
    return lax.ppermute(value, axis, pairs)


def ring_pairs(replica_count, pipe_count):
    pairs = []
    for replica in range(replica_count):
        for rank in range(pipe_count):
            step = 1 if rank >= pipe_count // 2 else 0
            target = ((replica + step) % replica_count) * pipe_count + pipe_count - 1 - rank
            pairs.append((replica * pipe_count + rank, target))
    return pairs


def ring_pass(value, pairs):
    moved = lax.ppermute(value.astype(jnp.bfloat16), ("dp", "pipe"), pairs)
    return moved.astype(jnp.float32)


def pre_act(field, gain, offset):
    channels, places = field.shape
    grouped = field.reshape(channels // (C // GROUPS), -1)
    centred = grouped - jnp.mean(grouped, axis=1, keepdims=True)
    spread = jnp.mean(centred * centred, axis=1, keepdims=True)
    normed = (centred * lax.rsqrt(spread + EPSILON)).reshape(channels, places)
    return jax.nn.silu(normed * gain[:, None] + offset[:, None])


def tap_stack(field):
    places = field.shape[1]
    plane = HT * WD
    margin = plane + WD + 1
    padded = jnp.pad(field, ((0, 0), (margin, margin)))
    position = jnp.arange(places, dtype=jnp.int32)
    frame_at = position // plane
    line_at = position // WD % HT
    column_at = position % WD
    pieces = []
    for shift_f in (-1, 0, 1):
        for shift_h in (-1, 0, 1):
            for shift_w in (-1, 0, 1):
                offset = shift_f * plane + shift_h * WD + shift_w
                inside = (frame_at + shift_f >= 0) & (frame_at + shift_f < FR)
                inside = inside & (line_at + shift_h >= 0) & (line_at + shift_h < HT)
                inside = inside & (column_at + shift_w >= 0) & (column_at + shift_w < WD)
                moved = lax.slice_in_dim(padded, margin + offset, margin + offset + places, axis=1)
                pieces.append(jnp.where(inside[None, :], moved, jnp.zeros_like(moved)))
    return jnp.concatenate(pieces, axis=0)


def tap_adjoint(grads, channels, places):
    pull = jax.vjp(tap_stack, jnp.zeros((channels, places), jnp.float32))[1]
    return pull(grads)[0]


def partial_term(weight_rows, front):
    return lax.dot_general(
        weight_rows, front, (((0,), (0,)), ((), ())), preferred_element_type=jnp.float32
    )


def conv_sums(rows_pair, fronts_pair):
    count = lax.axis_size("chan")
    parts = jnp.stack(
        [
            partial_term(rows, front).astype(jnp.bfloat16)
            for rows, front in zip(rows_pair, fronts_pair)
        ]
    )
    parts = parts.reshape(parts.shape[0], count, parts.shape[1] // count, parts.shape[2])
    got = lax.all_to_all(parts, "chan", 1, 1, tiled=False)
    sums = jnp.sum(got.astype(jnp.float32), axis=1)
    return [sums[direction] for direction in range(sums.shape[0])]


def conv_sum_single(rows_pair, fronts_pair, first_live):
    count = lax.axis_size("chan")
    first, second = [
        partial_term(rows, front).astype(jnp.bfloat16)
        for rows, front in zip(rows_pair, fronts_pair)
    ]
    part = jnp.where(first_live, first, second)
    part = part.reshape(count, part.shape[0] // count, part.shape[1])
    got = lax.all_to_all(part, "chan", 0, 0, tiled=False)
    total = jnp.sum(got.astype(jnp.float32), axis=0)
    return [total, total]


def gather_single(grads_pair, live_pair):
    count = lax.axis_size("chan")
    merged = grads_pair[0] + grads_pair[1]
    spread = jnp.broadcast_to(merged[None], (count,) + merged.shape)
    got = lax.all_to_all(spread, "chan", 0, 0, tiled=False)
    got = got.reshape(count * got.shape[1], got.shape[2])
    return [jnp.where(live, got, jnp.zeros_like(got)) for live in live_pair]


def live_at(tick_index, rank, direction, pipe_count, half_slots, backward):
    section = rank if direction == 0 else pipe_count - 1 - rank
    lag = pipe_count - 1 - section if backward else section
    return 0 <= tick_index - lag < half_slots


def relay(values, tick_index, pipe_count, half_slots, backward):
    pair_lists = []
    for direction in range(2):
        step = (1 if direction == 0 else -1) * (-1 if backward else 1)
        pairs = []
        for rank in range(pipe_count):
            target = rank + step
            if 0 <= target < pipe_count and live_at(
                tick_index, rank, direction, pipe_count, half_slots, backward
            ):
                pairs.append((rank, target))
        pair_lists.append(pairs)
    union = pair_lists[0] + pair_lists[1]
    sources = [source for source, _ in union]
    targets = [target for _, target in union]
    if len(set(sources)) == len(union) and len(set(targets)) == len(union):
        if not union:
            return [jnp.zeros_like(values[0]), jnp.zeros_like(values[1])]
        first_sources = jnp.array([source for source, _ in pair_lists[0]] + [-1], jnp.int32)
        rank_now = lax.axis_index("pipe")
        picked = jnp.where(jnp.any(first_sources == rank_now), values[0], values[1])
        got = lax.ppermute(picked, "pipe", union)
        return [got, got]
    moved = []
    for direction in range(2):
        if pair_lists[direction]:
            moved.append(lax.ppermute(values[direction], "pipe", pair_lists[direction]))
        else:
            moved.append(jnp.zeros_like(values[direction]))
    return moved


def both_live(tick_index, pipe_count, half_slots, backward):
    for rank in range(pipe_count):
        first = tick_index - (pipe_count - 1 - rank if backward else rank)
        second = tick_index - (rank if backward else pipe_count - 1 - rank)
        if 0 <= first < half_slots and 0 <= second < half_slots:
            return True
    return False


def conv_one(rows, front):
    count = lax.axis_size("chan")
    part = partial_term(rows, front).astype(jnp.bfloat16)
    part = part.reshape(count, part.shape[0] // count, part.shape[1])
    got = lax.all_to_all(part, "chan", 0, 0, tiled=False)
    return jnp.sum(got.astype(jnp.float32), axis=0)


def gather_one(grad):
    count = lax.axis_size("chan")
    spread = jnp.broadcast_to(grad[None], (count,) + grad.shape)
    got = lax.all_to_all(spread, "chan", 0, 0, tiled=False)
    return got.reshape(count * got.shape[1], got.shape[2])


def gather_pair(grads_pair):
    count = lax.axis_size("chan")
    stacked = jnp.stack(grads_pair)
    spread = jnp.broadcast_to(stacked[:, None], (stacked.shape[0], count) + stacked.shape[1:])
    got = lax.all_to_all(spread, "chan", 1, 1, tiled=False)
    got = got.reshape(got.shape[0], count * got.shape[2], got.shape[3])
    return [got[direction] for direction in range(got.shape[0])]


def fold_grads(grad_taps, grad_weight, piece, weight_rows, front):
    grad_taps = jnp.dot(weight_rows, piece, preferred_element_type=jnp.float32)
    previous = grad_weight
    update = lax.dot_general(
        front, piece, (((1,), (1,)), ((), ())), preferred_element_type=jnp.float32
    )
    grad_weight = previous + update
    return (grad_taps, grad_weight)


def grad_fold(full_grad, weight_rows, front, grad_weight):
    empty = jnp.zeros(front.shape, jnp.float32)
    return fold_grads(empty, grad_weight, full_grad, weight_rows, front)


def per_device(latents, cotangent, order, tstep, emb_table, gn_gain, weights):
    pipe_count = lax.axis_size("pipe")
    section_rank = lax.axis_index("pipe")
    mirror_rank = pipe_count - 1 - section_rank
    channels = latents.shape[2]
    places = latents.shape[3]
    slot_count = latents.shape[1]
    half_slots = slot_count // 2
    width = weights.shape[3]
    order_row = order[0]
    timestep_row = tstep[0]
    slot_ids = jnp.arange(slot_count, dtype=jnp.int32)
    picked = jnp.sum(
        jnp.where(order_row[:, None] == slot_ids[None, :], timestep_row[None, :], 0), axis=1
    )
    entries_all = jnp.take(latents[0], order_row, axis=0)
    sections = (section_rank, mirror_rank)
    rows_list = []
    gains = []
    offsets_list = []
    inputs = []
    cotans = []
    for direction in range(2):
        section = sections[direction]
        rows_list.append(
            lax.dynamic_index_in_dim(weights, section, 0, keepdims=False).reshape(
                27 * channels, width
            )
        )
        gains.append(lax.dynamic_index_in_dim(gn_gain, section, 0, keepdims=False))
        table = lax.dynamic_index_in_dim(emb_table, section, 1, keepdims=False)
        steps_now = picked[direction * half_slots : (direction + 1) * half_slots]
        offsets_list.append(jnp.take(table, steps_now, axis=0, mode="clip"))
        inputs.append(entries_all[direction * half_slots : (direction + 1) * half_slots])
        cotans.append(cotangent[0, direction * half_slots : (direction + 1) * half_slots])
    ticks = pipe_count + half_slots - 1
    zero_field = jnp.zeros((channels, places), jnp.bfloat16)
    received = [zero_field, zero_field]
    stores = [jnp.zeros((half_slots, channels, places), jnp.bfloat16) for direction in range(2)]
    rows_stack = jnp.stack(rows_list)
    for tick_index in range(ticks):
        entries_now = []
        offsets_now = []
        lives = []
        for direction in range(2):
            section = sections[direction]
            micro = tick_index - section
            is_live = (micro >= 0) & (micro < half_slots)
            lives.append(is_live)
            clipped = jnp.clip(micro, 0, half_slots - 1)
            fresh = lax.dynamic_index_in_dim(inputs[direction], clipped, 0, keepdims=False)
            entry = jnp.where(section == 0, fresh, received[direction])
            kept = lax.dynamic_index_in_dim(stores[direction], clipped, 0, keepdims=False)
            stores[direction] = lax.dynamic_update_index_in_dim(
                stores[direction], jnp.where(is_live, entry, kept), clipped, 0
            )
            offsets_now.append(
                lax.dynamic_index_in_dim(offsets_list[direction], clipped, 0, keepdims=False)
            )
            entries_now.append(entry)
        if both_live(tick_index, pipe_count, half_slots, False):
            fronts = [
                tap_stack(
                    pre_act(
                        entries_now[direction].astype(jnp.float32),
                        gains[direction],
                        offsets_now[direction],
                    ).astype(jnp.bfloat16)
                )
                for direction in range(2)
            ]
            sums = conv_sums(rows_list, fronts)
        else:
            pick = lives[0]
            entry = jnp.where(pick, entries_now[0], entries_now[1])
            gain = jnp.where(pick, gains[0], gains[1])
            offset = jnp.where(pick, offsets_now[0], offsets_now[1])
            rows = lax.dynamic_index_in_dim(rows_stack, jnp.where(pick, 0, 1), 0, keepdims=False)
            front = tap_stack(pre_act(entry.astype(jnp.float32), gain, offset).astype(jnp.bfloat16))
            total = conv_one(rows, front)
            sums = [total, total]
        results = [
            (entries_now[direction].astype(jnp.float32) + sums[direction]).astype(jnp.bfloat16)
            for direction in range(2)
        ]
        if tick_index + 1 < ticks:
            received = relay(results, tick_index, pipe_count, half_slots, False)
    grads_in = [zero_field, zero_field]
    acc_stack = jnp.zeros((2, 27 * channels, width), jnp.float32)
    for tick_index in range(ticks):
        live_grads = []
        entries_now = []
        offsets_now = []
        lives = []
        for direction in range(2):
            section = sections[direction]
            micro = tick_index - (pipe_count - 1 - section)
            is_live = (micro >= 0) & (micro < half_slots)
            lives.append(is_live)
            clipped = jnp.clip(micro, 0, half_slots - 1)
            fresh = lax.dynamic_index_in_dim(cotans[direction], clipped, 0, keepdims=False)
            incoming = jnp.where(section == pipe_count - 1, fresh, grads_in[direction])
            live_grads.append(jnp.where(is_live, incoming, zero_field))
            entries_now.append(lax.dynamic_index_in_dim(stores[direction], clipped, 0, keepdims=False))
            offsets_now.append(
                lax.dynamic_index_in_dim(offsets_list[direction], clipped, 0, keepdims=False)
            )
        sends = []
        if both_live(tick_index, pipe_count, half_slots, True):
            full_grads = gather_pair(live_grads)
            for direction in range(2):
                active, pull = jax.vjp(
                    partial(pre_act, gain=gains[direction], offset=offsets_now[direction]),
                    entries_now[direction].astype(jnp.float32),
                )
                front = tap_stack(active.astype(jnp.bfloat16))
                grad_taps, update = fold_grads(
                    None, 0.0, full_grads[direction], rows_list[direction], front
                )
                acc_stack = acc_stack.at[direction].add(update)
                back = pull(tap_adjoint(grad_taps, channels, places))[0]
                sends.append(
                    (live_grads[direction].astype(jnp.float32) + back).astype(jnp.bfloat16)
                )
        else:
            pick = lives[0]
            chosen = jnp.where(pick, 0, 1)
            entry = jnp.where(pick, entries_now[0], entries_now[1])
            gain = jnp.where(pick, gains[0], gains[1])
            offset = jnp.where(pick, offsets_now[0], offsets_now[1])
            active, pull = jax.vjp(partial(pre_act, gain=gain, offset=offset), entry.astype(jnp.float32))
            front = tap_stack(active.astype(jnp.bfloat16))
            full = gather_one(live_grads[0] + live_grads[1])
            rows = lax.dynamic_index_in_dim(rows_stack, chosen, 0, keepdims=False)
            grad_taps, update = fold_grads(None, 0.0, full, rows, front)
            previous = lax.dynamic_index_in_dim(acc_stack, chosen, 0, keepdims=False)
            acc_stack = lax.dynamic_update_index_in_dim(acc_stack, previous + update, chosen, 0)
            back = pull(tap_adjoint(grad_taps, channels, places))[0]
            for direction in range(2):
                sends.append(
                    (live_grads[direction].astype(jnp.float32) + back).astype(jnp.bfloat16)
                )
        if tick_index + 1 < ticks:
            grads_in = relay(sends, tick_index, pipe_count, half_slots, True)
    accums = [acc_stack[0], acc_stack[1]]
    replica_count = lax.axis_size("dp")
    onward = ring_pairs(replica_count, pipe_count)
    backward_pairs = [(target, source) for source, target in onward]
    taps = accums[0].shape[0] // channels
    half = (taps + 1) // 2
    own, other = [accum.reshape(taps, channels, width) for accum in accums]
    own_a, own_b = own[:half], own[half:]
    other_a, other_b = other[:half], other[half:]
    from_pred = ring_pass(jnp.concatenate([own_a, other_b], axis=0), onward)
    from_succ = ring_pass(jnp.concatenate([other_a, own_b], axis=0), backward_pairs)
    own_a = own_a + from_succ[:half]
    other_a = other_a + from_pred[:half]
    own_b = own_b + from_pred[half:]
    other_b = other_b + from_succ[half:]
    final_a = own_a + ring_pass(other_a, onward)
    final_b = own_b + ring_pass(other_b, backward_pairs)
    total = jnp.concatenate([final_a, final_b], axis=0)
    return total.reshape(1, 27, channels, width)


def solution(mesh):
    return jax.shard_map(
        per_device,
        mesh=mesh,
        in_specs=(
            P("dp", None, "chan", None),
            P("dp", None, "chan", None),
            P("dp", None),
            P("dp", None),
            P(None, None, "chan"),
            P(None, "chan"),
            P(None, None, "chan", None),
        ),
        out_specs=P("pipe", None, "chan", None),
        check_vma=False,
    )
```
